32 devices in a mesh: grp: 8 (over z, x), split: 4 (over y, core).
Axes of the slice: x: 2, y: 2, z: 4, core: 2. Of those that a mesh axis runs over, the one named last changes fastest.
Arguments:
- states: bfloat16 [12288, 4096], P(('grp', 'split'))
- weight: bfloat16 [4096, 1024], replicated, may hold values from -0.09375 to 0.09375
- cluster_id: int32 [12288], P(('grp', 'split')), may hold values from 0 to 31, as said below
- block: int32 [12288], P(('grp', 'split')), may hold values from 0 to 3
- order: int32 [12288], P(('grp', 'split')), may hold values from 0 to 12287, each once
Outputs:
- maxcos: float32 [12288], P(('grp', 'split'))
The draws below stay inside these ranges and needn't reach their ends.
Inputs may be any that keep to these rules, and one draw needn't show every extreme that they name: Cluster c is owned by group c // 4; the pair (cluster_id // 4, block) names a device of the mesh; at most 24 documents of one device go to one such device, and in every draw some devices take exactly 24 documents from every device. `order`: distinct over all documents.
All inputs are finite; a program needn't handle non-finite values.
Results may differ from the reference program's by a relative error of at most 0.0003.
Values may be sent and summed in bfloat16 or wider, within the bound.
No kernel may reach another device: no remote copies, remote signals or barrier semaphores. Data moves between devices by JAX's collectives and lax.ppermute only.
A program may use at most 64 MiB of HBM per device.

```python
import jax
import jax.numpy as jnp
from jax import lax

H = 4096
E = 1024
DOC_DEV = 384
CL_GRP = 4
MOTIFS = 16
CAP = 24
DOCS = 12288
N_GRP = 8
N_SPLIT = 4


def layout(key):
    ndev = N_GRP * N_SPLIT
    slots = ndev * CAP
    hot_n = max(1, DOC_DEV // (2 * CAP))
    hot = jax.random.permutation(jax.random.fold_in(key, 102), ndev)[:hot_n]
    is_hot = jnp.zeros((ndev,), jnp.int32).at[hot].set(1)
    keys = jax.random.split(jax.random.fold_in(key, 103), ndev)
    base = jax.vmap(lambda k: jax.random.permutation(k, slots))(keys).astype(jnp.int32)
    score = base + slots * jnp.repeat(is_hot, CAP)[None, :]
    chosen = jnp.argsort(-score, axis=1)[:, :DOC_DEV].astype(jnp.int32)
    mix_keys = jax.random.split(jax.random.fold_in(key, 104), ndev)
    shuffle = jax.vmap(lambda k: jax.random.permutation(k, DOC_DEV))(mix_keys).astype(jnp.int32)
    chosen = jnp.take_along_axis(chosen, shuffle, axis=1)
    target = (chosen // CAP).reshape(-1)
    pick = jax.random.randint(jax.random.fold_in(key, 105), (ndev * DOC_DEV,), 0, CL_GRP).astype(jnp.int32)
    cluster = target // N_SPLIT * CL_GRP + pick
    block = target % N_SPLIT
    return (cluster.astype(jnp.int32), block.astype(jnp.int32))


def draw_cluster_id(key, part):
    return layout(key)[0]


def draw_block(key, part):
    return layout(key)[1]


def draw_states(key, part):
    cluster = layout(key)[0]
    nclust = CL_GRP * N_GRP
    theme = jax.random.randint(jax.random.fold_in(key, 106), (DOCS,), 0, MOTIFS).astype(jnp.int32)
    centers = jax.random.normal(jax.random.fold_in(key, 107), (nclust, H), jnp.float32)
    motifs = jax.random.normal(jax.random.fold_in(key, 108), (nclust * MOTIFS, H), jnp.float32)
    strength = jax.random.uniform(jax.random.fold_in(key, 109), (DOCS, 1), jnp.float32, 0.2, 1.2)
    noise = jax.random.normal(jax.random.fold_in(key, 110), (DOCS, H), jnp.float32)
    rows = 0.5 * centers[cluster] + strength * motifs[cluster * MOTIFS + theme] + 0.6 * noise
    return rows.astype(jnp.bfloat16)


def normal_values(own_key, shape, deviation, most, kind=jnp.bfloat16):
    values = jax.random.normal(own_key, shape, jnp.float32) * deviation
    return jnp.minimum(jnp.maximum(values, -most), most).astype(kind)


def setup_inputs(seed: int = 0) -> dict:
    streams_of = jax.random.split(jax.random.key(seed), 6)
    return {
        "states": draw_states(jax.random.fold_in(streams_of[5], 71), 0),
        "weight": normal_values(streams_of[1], (H, E), H ** -0.5, 0.09375),
        "cluster_id": draw_cluster_id(jax.random.fold_in(streams_of[5], 71), 0),
        "block": draw_block(jax.random.fold_in(streams_of[5], 71), 0),
        "order": jax.random.permutation(streams_of[4], DOCS).astype(jnp.int32),
    }


EPS = 1e-06

def embed_rows(rows, weight):
    proj = jnp.dot(rows.astype(jnp.float32), weight.astype(jnp.float32), precision=lax.Precision.HIGHEST)
    scale = lax.rsqrt(lax.optimization_barrier(jnp.sum(proj * proj, axis=-1, keepdims=True)) + EPS)
    return (proj * scale).astype(jnp.bfloat16)

def reference(states, weight, cluster_id, block, order):
    ndocs = states.shape[0]
    devices = N_GRP * N_SPLIT
    stacked = states.reshape(devices, ndocs // devices, states.shape[1])
    embeds = lax.map(lambda rows: embed_rows(rows, weight), stacked).reshape(ndocs, -1)
    group = (cluster_id // CL_GRP).astype(jnp.int32)
    rank = (block * ndocs + order).astype(jnp.int32)
    index = jnp.argsort(group, stable=True).astype(jnp.int32)
    counts = lax.optimization_barrier(jnp.sum((group[None, :] == jnp.arange(N_GRP, dtype=jnp.int32)[:, None]).astype(jnp.int32), axis=1))
    starts = (jnp.cumsum(counts) - counts).astype(jnp.int32)
    slab = N_SPLIT * devices * CAP
    emb_sorted = jnp.concatenate([embeds[index], jnp.zeros((slab, embeds.shape[1]), jnp.bfloat16)], axis=0)
    lab_sorted = jnp.concatenate([cluster_id[index], jnp.full((slab,), -1, jnp.int32)], axis=0)
    rank_sorted = jnp.concatenate([rank[index], jnp.zeros((slab,), jnp.int32)], axis=0)
    idx_sorted = jnp.concatenate([index, jnp.full((slab,), ndocs, jnp.int32)], axis=0)
    positions = jnp.arange(slab, dtype=jnp.int32)

    def per_group(g):
        start = starts[g]
        emb = lax.dynamic_slice_in_dim(emb_sorted, start, slab, 0).astype(jnp.float32)
        lab = lax.dynamic_slice_in_dim(lab_sorted, start, slab, 0)
        rnk = lax.dynamic_slice_in_dim(rank_sorted, start, slab, 0)
        who = lax.dynamic_slice_in_dim(idx_sorted, start, slab, 0)
        valid = positions < counts[g]
        scores = jnp.dot(emb, emb.T, precision=lax.Precision.HIGHEST)
        hits = (lab[:, None] == lab[None, :]) & (rnk[None, :] < rnk[:, None]) & valid[None, :]
        best = lax.optimization_barrier(jnp.max(jnp.where(hits, scores, jnp.float32(-1.0)), axis=1))
        best = jnp.maximum(best, jnp.float32(-1.0))
        target = jnp.where(valid, who, ndocs).astype(jnp.int32)
        return (best, target)
    best, target = lax.map(per_group, jnp.arange(N_GRP, dtype=jnp.int32))
    out = jnp.zeros((ndocs,), jnp.float32).at[target.reshape(-1)].set(best.reshape(-1), mode='drop')
    return out
```

```python
import jax
import jax.numpy as jnp
from jax import lax
from jax.sharding import PartitionSpec as P

CL_GRP = 4


EPS = 1e-06
META = 128


def embed_rows(rows, weight):
    proj = jnp.einsum("...h,he->...e", rows, weight, preferred_element_type=jnp.float32)
    scale = lax.rsqrt(jnp.sum(proj * proj, axis=-1, keepdims=True) + EPS)
    return (proj * scale).astype(jnp.bfloat16)


def shift_keys(keys, n_split):
    if n_split == 4:
        up = lax.ppermute(keys, "split", [(0, 2), (1, 3)])
        near = lax.ppermute(keys, "split", [(0, 1), (2, 3)])
        swap = lax.ppermute(up, "split", [(2, 3), (3, 2)])
        return [up, near, swap]
    out = []
    for d in range(1, n_split):
        route = [(i - d, i) for i in range(d, n_split)]
        out.append(lax.ppermute(keys, "split", route))
    return out


def unpack(buf, emb_w):
    emb = buf[:, :emb_w]
    lab = buf[:, emb_w].astype(jnp.float32)
    order = buf[:, emb_w + 1].astype(jnp.float32) * 256.0 + buf[:, emb_w + 2].astype(jnp.float32)
    return emb, lab, order


def local(states, weight, cluster_id, block, order):
    n_doc = states.shape[0]
    n_grp = lax.axis_size("grp")
    n_split = lax.axis_size("split")
    n_dev = n_grp * n_split
    cap = max(2, 2 * n_doc // n_dev)
    n_slot = n_dev * cap
    owner_of = cluster_id // CL_GRP
    target = owner_of * n_split + block
    onehot = (target[:, None] == jnp.arange(n_dev, dtype=jnp.int32)[None, :]).astype(jnp.bfloat16)
    lower = (jnp.arange(n_doc)[:, None] > jnp.arange(n_doc)[None, :]).astype(jnp.bfloat16)
    before = jnp.dot(lower, onehot, preferred_element_type=jnp.float32)
    slot = jnp.sum(before * onehot.astype(jnp.float32), axis=1).astype(jnp.int32)
    place = target * cap + slot

    embeds = embed_rows(states, weight)
    emb_w = embeds.shape[1]
    label = (cluster_id - owner_of * CL_GRP + 1).astype(jnp.float32)
    meta_cols = jnp.stack(
        [label, (order // 256).astype(jnp.float32), (order % 256).astype(jnp.float32)], axis=1
    )
    meta = jnp.concatenate(
        [meta_cols, jnp.zeros((n_doc, META - meta_cols.shape[1]), jnp.float32)], axis=1
    ).astype(jnp.bfloat16)
    rows = jnp.concatenate([embeds, meta], axis=1)
    pick = place[None, :] == jnp.arange(n_slot, dtype=jnp.int32)[:, None]
    send = jnp.dot(pick.astype(jnp.bfloat16), rows, preferred_element_type=jnp.float32).astype(
        jnp.bfloat16
    )
    got = lax.all_to_all(
        send.reshape(n_dev, cap, -1), ("grp", "split"), split_axis=0, concat_axis=0, tiled=True
    ).reshape(n_slot, -1)

    q_emb, q_lab, q_ord = unpack(got, emb_w)
    scores = jnp.einsum("qe,ke->qk", q_emb, q_emb, preferred_element_type=jnp.float32)
    hits = (q_lab[:, None] == q_lab[None, :]) & (q_lab[None, :] > 0) & (q_ord[None, :] < q_ord[:, None])
    best = jnp.max(jnp.where(hits, scores, jnp.float32(-1.0)), axis=1)
    for keys in shift_keys(got, n_split):
        k_emb, k_lab, _ = unpack(keys, emb_w)
        scores = jnp.einsum("qe,ke->qk", q_emb, k_emb, preferred_element_type=jnp.float32)
        hits = (q_lab[:, None] == k_lab[None, :]) & (k_lab[None, :] > 0)
        best = jnp.maximum(best, jnp.max(jnp.where(hits, scores, jnp.float32(-1.0)), axis=1))

    returned = lax.all_to_all(
        best.reshape(n_dev, cap), ("grp", "split"), split_axis=0, concat_axis=0, tiled=True
    ).reshape(n_slot)
    return jnp.max(jnp.where(pick, returned[:, None], -jnp.inf), axis=0)


def solution(mesh):
    in_specs = (
        P(("grp", "split"), None),
        P(),
        P(("grp", "split")),
        P(("grp", "split")),
        P(("grp", "split")),
    )
    out_specs = P(("grp", "split"))
    return jax.shard_map(local, mesh=mesh, in_specs=in_specs, out_specs=out_specs, check_vma=False)
```

```python
import jax
import jax.numpy as jnp
from jax import lax
from jax.sharding import PartitionSpec as P

CL_GRP = 4


EPS = 1e-06
META = 128


def embed_rows(rows, weight):
    proj = jnp.einsum("...h,he->...e", rows, weight, preferred_element_type=jnp.float32)
    scale = lax.rsqrt(jnp.sum(proj * proj, axis=-1, keepdims=True) + EPS)
    return (proj * scale).astype(jnp.bfloat16)


def shift_keys(keys, n_split):
    if n_split == 4:
        up = lax.ppermute(keys, "split", [(0, 2), (1, 3)])
        near = lax.ppermute(keys, "split", [(0, 1), (2, 3)])
        swap = lax.ppermute(up, "split", [(2, 3), (3, 2)])
        return [up, near, swap]
    out = []
    for d in range(1, n_split):
        route = [(i - d, i) for i in range(d, n_split)]
        out.append(lax.ppermute(keys, "split", route))
    return out


def unpack(buf, emb_w):
    emb = buf[:, :emb_w]
    lab = buf[:, emb_w].astype(jnp.float32)
    order = buf[:, emb_w + 1].astype(jnp.float32) * 256.0 + buf[:, emb_w + 2].astype(jnp.float32)
    return emb, lab, order


def local(states, weight, cluster_id, block, order):
    n_doc = states.shape[0]
    n_grp = lax.axis_size("grp")
    n_split = lax.axis_size("split")
    n_dev = n_grp * n_split
    cap = max(2, 2 * n_doc // n_dev)
    n_slot = n_dev * cap
    owner_of = cluster_id // CL_GRP
    target = owner_of * n_split + block
    onehot = (target[:, None] == jnp.arange(n_dev, dtype=jnp.int32)[None, :]).astype(jnp.bfloat16)
    lower = (jnp.arange(n_doc)[:, None] > jnp.arange(n_doc)[None, :]).astype(jnp.bfloat16)
    before = jnp.dot(lower, onehot, preferred_element_type=jnp.float32)
    slot = jnp.sum(before * onehot.astype(jnp.float32), axis=1).astype(jnp.int32)
    place = target * cap + slot

    embeds = embed_rows(states, weight)
    emb_w = embeds.shape[1]
    half = emb_w // 2
    label = (cluster_id - owner_of * CL_GRP + 1).astype(jnp.float32)
    meta_cols = jnp.stack(
        [label, (order // 256).astype(jnp.float32), (order % 256).astype(jnp.float32)], axis=1
    )
    meta = jnp.concatenate(
        [meta_cols, jnp.zeros((n_doc, META - meta_cols.shape[1]), jnp.float32)], axis=1
    ).astype(jnp.bfloat16)
    pick = place[None, :] == jnp.arange(n_slot, dtype=jnp.int32)[:, None]

    def route(rows):
        send = jnp.dot(pick.astype(jnp.bfloat16), rows, preferred_element_type=jnp.float32)
        send = send.astype(jnp.bfloat16).reshape(n_dev, cap, -1)
        got = lax.all_to_all(send, ("grp", "split"), split_axis=0, concat_axis=0, tiled=True)
        return got.reshape(n_slot, -1)

    got_a = route(jnp.concatenate([embeds[:, :half], meta], axis=1))
    keys_a = shift_keys(got_a, n_split)
    got_b = route(embeds[:, half:])
    keys_b = shift_keys(got_b, n_split)

    q_emb, q_lab, q_ord = unpack(got_a, half)

    def dots(k_a, k_b):
        s = jnp.einsum("qe,ke->qk", q_emb, k_a[:, :half], preferred_element_type=jnp.float32)
        return s + jnp.einsum("qe,ke->qk", got_b, k_b, preferred_element_type=jnp.float32)

    scores = dots(got_a, got_b)
    hits = (q_lab[:, None] == q_lab[None, :]) & (q_lab[None, :] > 0) & (q_ord[None, :] < q_ord[:, None])
    best = jnp.max(jnp.where(hits, scores, jnp.float32(-1.0)), axis=1)
    for k_a, k_b in zip(keys_a, keys_b):
        _, k_lab, _ = unpack(k_a, half)
        scores = dots(k_a, k_b)
        hits = (q_lab[:, None] == k_lab[None, :]) & (k_lab[None, :] > 0)
        best = jnp.maximum(best, jnp.max(jnp.where(hits, scores, jnp.float32(-1.0)), axis=1))

    returned = lax.all_to_all(
        best.reshape(n_dev, cap), ("grp", "split"), split_axis=0, concat_axis=0, tiled=True
    ).reshape(n_slot)
    return jnp.max(jnp.where(pick, returned[:, None], -jnp.inf), axis=0)


def solution(mesh):
    in_specs = (
        P(("grp", "split"), None),
        P(),
        P(("grp", "split")),
        P(("grp", "split")),
        P(("grp", "split")),
    )
    out_specs = P(("grp", "split"))
    return jax.shard_map(local, mesh=mesh, in_specs=in_specs, out_specs=out_specs, check_vma=False)
```

```python
import jax
import jax.numpy as jnp
from jax import lax
from jax.sharding import PartitionSpec as P

CL_GRP = 4


EPS = 1e-06
META = 128


def embed_rows(rows, weight):
    proj = jnp.einsum("...h,he->...e", rows, weight, preferred_element_type=jnp.float32)
    scale = lax.rsqrt(jnp.sum(proj * proj, axis=-1, keepdims=True) + EPS)
    return (proj * scale).astype(jnp.bfloat16)


def gather_split(rows, n_split):
    if n_split == 4:
        cross = lax.ppermute(rows, "split", [(0, 2), (1, 3), (2, 0), (3, 1)])
        pair = [(0, 1), (1, 0), (2, 3), (3, 2)]
        return [cross, lax.ppermute(rows, "split", pair), lax.ppermute(cross, "split", pair)]
    return [
        lax.ppermute(rows, "split", [(i, (i + d) % n_split) for i in range(n_split)])
        for d in range(1, n_split)
    ]


def unpack(buf, emb_w, n_all):
    emb = buf[:, :emb_w]
    lab = buf[:, emb_w].astype(jnp.float32)
    digits = [buf[:, emb_w + i].astype(jnp.float32) for i in (1, 2, 3)]
    return emb, lab, (digits[0] * n_all + digits[1] * 256.0) + digits[2]


def local(states, weight, cluster_id, block, order):
    n_doc = states.shape[0]
    n_grp = lax.axis_size("grp")
    n_split = lax.axis_size("split")
    n_dev = n_grp * n_split
    n_all = n_doc * n_dev
    cap = n_split * max(2, 2 * n_doc // n_dev)
    n_slot = n_grp * cap
    owner_of = cluster_id // CL_GRP
    onehot = (owner_of[:, None] == jnp.arange(n_grp, dtype=jnp.int32)[None, :]).astype(jnp.bfloat16)
    lower = (jnp.arange(n_doc)[:, None] > jnp.arange(n_doc)[None, :]).astype(jnp.bfloat16)
    before = jnp.dot(lower, onehot, preferred_element_type=jnp.float32)
    slot = jnp.sum(before * onehot.astype(jnp.float32), axis=1).astype(jnp.int32)
    place = owner_of * cap + slot

    embeds = embed_rows(states, weight)
    emb_w = embeds.shape[1]
    half = emb_w // 2
    label = (cluster_id - owner_of * CL_GRP + 1).astype(jnp.float32)
    meta_cols = jnp.stack(
        [label, block.astype(jnp.float32), (order // 256).astype(jnp.float32),
         (order % 256).astype(jnp.float32)],
        axis=1,
    )
    meta = jnp.concatenate(
        [meta_cols, jnp.zeros((n_doc, META - meta_cols.shape[1]), jnp.float32)], axis=1
    ).astype(jnp.bfloat16)
    pick = place[None, :] == jnp.arange(n_slot, dtype=jnp.int32)[:, None]

    def route(rows):
        send = jnp.dot(pick.astype(jnp.bfloat16), rows, preferred_element_type=jnp.float32)
        send = send.astype(jnp.bfloat16).reshape(n_grp, cap, -1)
        got = lax.all_to_all(send, "grp", split_axis=0, concat_axis=0, tiled=True)
        return got.reshape(n_slot, -1)

    got_a = route(jnp.concatenate([embeds[:, :half], meta], axis=1))
    keys_a = gather_split(got_a, n_split)
    got_b = route(embeds[:, half:])
    keys_b = gather_split(got_b, n_split)

    q_emb, q_lab, q_ord = unpack(got_a, half, n_all)

    def dots(k_a, k_b):
        s = jnp.einsum("qe,ke->qk", q_emb, k_a[:, :half], preferred_element_type=jnp.float32)
        return s + jnp.einsum("qe,ke->qk", got_b, k_b, preferred_element_type=jnp.float32)

    scores = dots(got_a, got_b)
    hits = (q_lab[:, None] == q_lab[None, :]) & (q_lab[None, :] > 0) & (q_ord[None, :] < q_ord[:, None])
    best = jnp.max(jnp.where(hits, scores, jnp.float32(-1.0)), axis=1)
    for k_a, k_b in zip(keys_a, keys_b):
        _, k_lab, k_ord = unpack(k_a, half, n_all)
        scores = dots(k_a, k_b)
        hits = (q_lab[:, None] == k_lab[None, :]) & (k_lab[None, :] > 0) & (k_ord[None, :] < q_ord[:, None])
        best = jnp.maximum(best, jnp.max(jnp.where(hits, scores, jnp.float32(-1.0)), axis=1))

    returned = lax.all_to_all(
        best.reshape(n_grp, cap), "grp", split_axis=0, concat_axis=0, tiled=True
    ).reshape(n_slot)
    return jnp.max(jnp.where(pick, returned[:, None], -jnp.inf), axis=0)


def solution(mesh):
    in_specs = (
        P(("grp", "split"), None),
        P(),
        P(("grp", "split")),
        P(("grp", "split")),
        P(("grp", "split")),
    )
    out_specs = P(("grp", "split"))
    return jax.shard_map(local, mesh=mesh, in_specs=in_specs, out_specs=out_specs, check_vma=False)
```

```python
import jax
import jax.numpy as jnp
from jax import lax
from jax.sharding import PartitionSpec as P

CL_GRP = 4


EPS = 1e-06
META = 128


def embed_rows(rows, weight):
    proj = jnp.einsum("...h,he->...e", rows, weight, preferred_element_type=jnp.float32)
    scale = lax.rsqrt(jnp.sum(proj * proj, axis=-1, keepdims=True) + EPS)
    return (proj * scale).astype(jnp.bfloat16)


def gather_split(rows, n_split):
    if n_split == 4:
        cross = lax.ppermute(rows, "split", [(0, 2), (1, 3), (2, 0), (3, 1)])
        pair = [(0, 1), (1, 0), (2, 3), (3, 2)]
        return [cross, lax.ppermute(rows, "split", pair), lax.ppermute(cross, "split", pair)]
    return [
        lax.ppermute(rows, "split", [(i, (i + d) % n_split) for i in range(n_split)])
        for d in range(1, n_split)
    ]


def unpack(buf, emb_w, n_all):
    emb = buf[:, :emb_w]
    lab = buf[:, emb_w].astype(jnp.float32)
    digits = [buf[:, emb_w + i].astype(jnp.float32) for i in (1, 2, 3)]
    return emb, lab, (digits[0] * n_all + digits[1] * 256.0) + digits[2]


def local(states, weight, cluster_id, block, order):
    n_doc = states.shape[0]
    n_grp = lax.axis_size("grp")
    n_split = lax.axis_size("split")
    n_dev = n_grp * n_split
    n_all = n_doc * n_dev
    cap = n_split * max(2, 2 * n_doc // n_dev)
    n_slot = n_grp * cap
    owner_of = cluster_id // CL_GRP
    onehot = (owner_of[:, None] == jnp.arange(n_grp, dtype=jnp.int32)[None, :]).astype(jnp.bfloat16)
    lower = (jnp.arange(n_doc)[:, None] > jnp.arange(n_doc)[None, :]).astype(jnp.bfloat16)
    before = jnp.dot(lower, onehot, preferred_element_type=jnp.float32)
    slot = jnp.sum(before * onehot.astype(jnp.float32), axis=1).astype(jnp.int32)
    place = owner_of * cap + slot

    embeds = embed_rows(states, weight)
    emb_w = embeds.shape[1]
    half = emb_w // 2
    label = (cluster_id - owner_of * CL_GRP + 1).astype(jnp.float32)
    meta_cols = jnp.stack(
        [label, block.astype(jnp.float32), (order // 256).astype(jnp.float32),
         (order % 256).astype(jnp.float32)],
        axis=1,
    )
    meta = jnp.concatenate(
        [meta_cols, jnp.zeros((n_doc, META - meta_cols.shape[1]), jnp.float32)], axis=1
    ).astype(jnp.bfloat16)
    pick = place[None, :] == jnp.arange(n_slot, dtype=jnp.int32)[:, None]

    def route(rows):
        send = jnp.dot(pick.astype(jnp.bfloat16), rows, preferred_element_type=jnp.float32)
        send = send.astype(jnp.bfloat16).reshape(n_grp, cap, -1)
        got = lax.all_to_all(send, "grp", split_axis=0, concat_axis=0, tiled=True)
        return got.reshape(n_slot, -1)

    got_a = route(jnp.concatenate([embeds[:, :half], meta], axis=1))
    q_emb, q_lab, q_ord = unpack(got_a, half, n_all)
    keys_a = gather_split(q_emb, n_split)
    keys_m = gather_split(jnp.stack([q_lab, q_ord]), n_split)
    got_b = route(embeds[:, half:])
    keys_b = gather_split(got_b, n_split)

    def dots(k_a, k_b):
        s = jnp.einsum("qe,ke->qk", q_emb, k_a, preferred_element_type=jnp.float32)
        return s + jnp.einsum("qe,ke->qk", got_b, k_b, preferred_element_type=jnp.float32)

    scores = dots(q_emb, got_b)
    hits = (q_lab[:, None] == q_lab[None, :]) & (q_lab[None, :] > 0) & (q_ord[None, :] < q_ord[:, None])
    best = jnp.max(jnp.where(hits, scores, jnp.float32(-1.0)), axis=1)
    for k_a, k_b, k_m in zip(keys_a, keys_b, keys_m):
        k_lab, k_ord = k_m[0], k_m[1]
        scores = dots(k_a, k_b)
        hits = (q_lab[:, None] == k_lab[None, :]) & (k_lab[None, :] > 0) & (k_ord[None, :] < q_ord[:, None])
        best = jnp.maximum(best, jnp.max(jnp.where(hits, scores, jnp.float32(-1.0)), axis=1))

    returned = lax.all_to_all(
        best.reshape(n_grp, cap), "grp", split_axis=0, concat_axis=0, tiled=True
    ).reshape(n_slot)
    return jnp.max(jnp.where(pick, returned[:, None], -jnp.inf), axis=0)


def solution(mesh):
    in_specs = (
        P(("grp", "split"), None),
        P(),
        P(("grp", "split")),
        P(("grp", "split")),
        P(("grp", "split")),
    )
    out_specs = P(("grp", "split"))
    return jax.shard_map(local, mesh=mesh, in_specs=in_specs, out_specs=out_specs, check_vma=False)
```

```python
import jax
import jax.numpy as jnp
from jax import lax
from jax.sharding import PartitionSpec as P

CL_GRP = 4


EPS = 1e-06
META = 128


def embed_rows(rows, weight):
    proj = jnp.einsum("...h,he->...e", rows, weight, preferred_element_type=jnp.float32)
    scale = lax.rsqrt(jnp.sum(proj * proj, axis=-1, keepdims=True) + EPS)
    return (proj * scale).astype(jnp.bfloat16)


def gather_split(rows, n_split):
    if n_split == 4:
        cross = lax.ppermute(rows, "split", [(0, 2), (1, 3), (2, 0), (3, 1)])
        pair = [(0, 1), (1, 0), (2, 3), (3, 2)]
        return [cross, lax.ppermute(rows, "split", pair), lax.ppermute(cross, "split", pair)]
    return [
        lax.ppermute(rows, "split", [(i, (i + d) % n_split) for i in range(n_split)])
        for d in range(1, n_split)
    ]


def unpack(buf, emb_w, n_all):
    emb = buf[:, :emb_w]
    lab = buf[:, emb_w].astype(jnp.float32)
    digits = [buf[:, emb_w + i].astype(jnp.float32) for i in (1, 2, 3)]
    return emb, lab, (digits[0] * n_all + digits[1] * 256.0) + digits[2]


def local(states, weight, cluster_id, block, order):
    n_doc = states.shape[0]
    n_grp = lax.axis_size("grp")
    n_split = lax.axis_size("split")
    n_dev = n_grp * n_split
    n_all = n_doc * n_dev
    cap = n_split * max(2, 2 * n_doc // n_dev)
    n_slot = n_grp * cap
    owner_of = cluster_id // CL_GRP
    onehot = (owner_of[:, None] == jnp.arange(n_grp, dtype=jnp.int32)[None, :]).astype(jnp.bfloat16)
    lower = (jnp.arange(n_doc)[:, None] > jnp.arange(n_doc)[None, :]).astype(jnp.bfloat16)
    before = jnp.dot(lower, onehot, preferred_element_type=jnp.float32)
    slot = jnp.sum(before * onehot.astype(jnp.float32), axis=1).astype(jnp.int32)
    place = owner_of * cap + slot

    embeds = embed_rows(states, weight)
    emb_w = embeds.shape[1]
    half = emb_w - 3 * emb_w // 8
    label = (cluster_id - owner_of * CL_GRP + 1).astype(jnp.float32)
    meta_cols = jnp.stack(
        [label, block.astype(jnp.float32), (order // 256).astype(jnp.float32),
         (order % 256).astype(jnp.float32)],
        axis=1,
    )
    meta = jnp.concatenate(
        [meta_cols, jnp.zeros((n_doc, META - meta_cols.shape[1]), jnp.float32)], axis=1
    ).astype(jnp.bfloat16)
    pick = place[None, :] == jnp.arange(n_slot, dtype=jnp.int32)[:, None]

    def route(rows):
        send = jnp.dot(pick.astype(jnp.bfloat16), rows, preferred_element_type=jnp.float32)
        send = send.astype(jnp.bfloat16).reshape(n_grp, cap, -1)
        got = lax.all_to_all(send, "grp", split_axis=0, concat_axis=0, tiled=True)
        return got.reshape(n_slot, -1)

    got_a = route(jnp.concatenate([embeds[:, :half], meta], axis=1))
    q_emb, q_lab, q_ord = unpack(got_a, half, n_all)
    keys_a = gather_split(q_emb, n_split)
    keys_m = gather_split(jnp.stack([q_lab, q_ord]), n_split)
    got_b = route(embeds[:, half:])
    keys_b = gather_split(got_b, n_split)

    def dots(k_a, k_b):
        s = jnp.einsum("qe,ke->qk", q_emb, k_a, preferred_element_type=jnp.float32)
        return s + jnp.einsum("qe,ke->qk", got_b, k_b, preferred_element_type=jnp.float32)

    scores = dots(q_emb, got_b)
    hits = (q_lab[:, None] == q_lab[None, :]) & (q_lab[None, :] > 0) & (q_ord[None, :] < q_ord[:, None])
    best = jnp.max(jnp.where(hits, scores, jnp.float32(-1.0)), axis=1)
    for k_a, k_b, k_m in zip(keys_a, keys_b, keys_m):
        k_lab, k_ord = k_m[0], k_m[1]
        scores = dots(k_a, k_b)
        hits = (q_lab[:, None] == k_lab[None, :]) & (k_lab[None, :] > 0) & (k_ord[None, :] < q_ord[:, None])
        best = jnp.maximum(best, jnp.max(jnp.where(hits, scores, jnp.float32(-1.0)), axis=1))

    returned = lax.all_to_all(
        best.reshape(n_grp, cap), "grp", split_axis=0, concat_axis=0, tiled=True
    ).reshape(n_slot)
    return jnp.max(jnp.where(pick, returned[:, None], -jnp.inf), axis=0)


def solution(mesh):
    in_specs = (
        P(("grp", "split"), None),
        P(),
        P(("grp", "split")),
        P(("grp", "split")),
        P(("grp", "split")),
    )
    out_specs = P(("grp", "split"))
    return jax.shard_map(local, mesh=mesh, in_specs=in_specs, out_specs=out_specs, check_vma=False)
```

```python
import jax
import jax.numpy as jnp
from jax import lax
from jax.sharding import PartitionSpec as P

CL_GRP = 4


EPS = 1e-06
META = 128


def embed_rows(rows, weight):
    proj = jnp.einsum("...h,he->...e", rows, weight, preferred_element_type=jnp.float32)
    scale = lax.rsqrt(jnp.sum(proj * proj, axis=-1, keepdims=True) + EPS)
    return (proj * scale).astype(jnp.bfloat16)


def gather_split(rows, n_split):
    if n_split == 4:
        cross = lax.ppermute(rows, "split", [(0, 2), (1, 3), (2, 0), (3, 1)])
        pair = [(0, 1), (1, 0), (2, 3), (3, 2)]
        return [cross, lax.ppermute(rows, "split", pair), lax.ppermute(cross, "split", pair)]
    return [
        lax.ppermute(rows, "split", [(i, (i + d) % n_split) for i in range(n_split)])
        for d in range(1, n_split)
    ]


def unpack(buf, emb_w, n_all):
    emb = buf[:, :emb_w]
    lab = buf[:, emb_w].astype(jnp.float32)
    digits = [buf[:, emb_w + i].astype(jnp.float32) for i in (1, 2, 3)]
    return emb, lab, (digits[0] * n_all + digits[1] * 256.0) + digits[2]


def local(states, weight, cluster_id, block, order):
    n_doc = states.shape[0]
    n_grp = lax.axis_size("grp")
    n_split = lax.axis_size("split")
    n_dev = n_grp * n_split
    n_all = n_doc * n_dev
    cap = n_split * max(2, 2 * n_doc // n_dev)
    n_slot = n_grp * cap
    owner_of = cluster_id // CL_GRP
    onehot = (owner_of[:, None] == jnp.arange(n_grp, dtype=jnp.int32)[None, :]).astype(jnp.bfloat16)
    lower = (jnp.arange(n_doc)[:, None] > jnp.arange(n_doc)[None, :]).astype(jnp.bfloat16)
    before = jnp.dot(lower, onehot, preferred_element_type=jnp.float32)
    slot = jnp.sum(before * onehot.astype(jnp.float32), axis=1).astype(jnp.int32)
    place = owner_of * cap + slot

    embeds = embed_rows(states, weight)
    emb_w = embeds.shape[1]
    half = emb_w // 2
    label = (cluster_id - owner_of * CL_GRP + 1).astype(jnp.float32)
    meta_cols = jnp.stack(
        [label, block.astype(jnp.float32), (order // 256).astype(jnp.float32),
         (order % 256).astype(jnp.float32)],
        axis=1,
    )
    meta = jnp.concatenate(
        [meta_cols, jnp.zeros((n_doc, META - meta_cols.shape[1]), jnp.float32)], axis=1
    ).astype(jnp.bfloat16)
    pick = place[None, :] == jnp.arange(n_slot, dtype=jnp.int32)[:, None]

    def route(rows):
        send = jnp.dot(pick.astype(jnp.bfloat16), rows, preferred_element_type=jnp.float32)
        send = send.astype(jnp.bfloat16).reshape(n_grp, cap, -1)
        got = lax.all_to_all(send, "grp", split_axis=0, concat_axis=0, tiled=True)
        return got.reshape(n_slot, -1)

    if n_split == 4:
        half = emb_w - 3 * emb_w // 8
        cross = [(0, 2), (2, 0), (1, 3), (3, 1)]
        pair = [(0, 1), (1, 0), (2, 3), (3, 2)]
        raw_b = embeds[:, half:]
        par_b = lax.ppermute(raw_b, "split", cross)
        par_place = lax.ppermute(place, "split", cross)
        got_a = route(jnp.concatenate([embeds[:, :half], meta], axis=1))
        q_emb, q_lab, q_ord = unpack(got_a, half, n_all)
        keys_a = gather_split(q_emb, n_split)
        keys_m = gather_split(jnp.stack([q_lab, q_ord]), n_split)
        pick_par = par_place[None, :] == jnp.arange(n_slot, dtype=jnp.int32)[:, None]
        send_own = jnp.dot(pick.astype(jnp.bfloat16), raw_b, preferred_element_type=jnp.float32)
        send_par = jnp.dot(pick_par.astype(jnp.bfloat16), par_b, preferred_element_type=jnp.float32)
        send = jnp.concatenate(
            [send_own.reshape(n_grp, cap, -1), send_par.reshape(n_grp, cap, -1)], axis=1
        ).astype(jnp.bfloat16)
        got = lax.all_to_all(send, "grp", split_axis=0, concat_axis=0, tiled=True)
        got_b = got[:, :cap].reshape(n_slot, -1)
        cross_b = got[:, cap:].reshape(n_slot, -1)
        keys_b = [cross_b, lax.ppermute(got_b, "split", pair), lax.ppermute(cross_b, "split", pair)]
    else:
        half = emb_w // 2
        got_a = route(jnp.concatenate([embeds[:, :half], meta], axis=1))
        q_emb, q_lab, q_ord = unpack(got_a, half, n_all)
        keys_a = gather_split(q_emb, n_split)
        keys_m = gather_split(jnp.stack([q_lab, q_ord]), n_split)
        got_b = route(embeds[:, half:])
        keys_b = gather_split(got_b, n_split)

    def dots(k_a, k_b):
        s = jnp.einsum("qe,ke->qk", q_emb, k_a, preferred_element_type=jnp.float32)
        return s + jnp.einsum("qe,ke->qk", got_b, k_b, preferred_element_type=jnp.float32)

    scores = dots(q_emb, got_b)
    hits = (q_lab[:, None] == q_lab[None, :]) & (q_lab[None, :] > 0) & (q_ord[None, :] < q_ord[:, None])
    best = jnp.max(jnp.where(hits, scores, jnp.float32(-1.0)), axis=1)
    for k_a, k_b, k_m in zip(keys_a, keys_b, keys_m):
        k_lab, k_ord = k_m[0], k_m[1]
        scores = dots(k_a, k_b)
        hits = (q_lab[:, None] == k_lab[None, :]) & (k_lab[None, :] > 0) & (k_ord[None, :] < q_ord[:, None])
        best = jnp.maximum(best, jnp.max(jnp.where(hits, scores, jnp.float32(-1.0)), axis=1))

    returned = lax.all_to_all(
        best.reshape(n_grp, cap), "grp", split_axis=0, concat_axis=0, tiled=True
    ).reshape(n_slot)
    return jnp.max(jnp.where(pick, returned[:, None], -jnp.inf), axis=0)


def solution(mesh):
    in_specs = (
        P(("grp", "split"), None),
        P(),
        P(("grp", "split")),
        P(("grp", "split")),
        P(("grp", "split")),
    )
    out_specs = P(("grp", "split"))
    return jax.shard_map(local, mesh=mesh, in_specs=in_specs, out_specs=out_specs, check_vma=False)
```

```python
import jax
import jax.numpy as jnp
from jax import lax
from jax.sharding import PartitionSpec as P

CL_GRP = 4


EPS = 1e-06
META = 128


def embed_rows(rows, weight):
    proj = jnp.einsum("...h,he->...e", rows, weight, preferred_element_type=jnp.float32)
    scale = lax.rsqrt(jnp.sum(proj * proj, axis=-1, keepdims=True) + EPS)
    return (proj * scale).astype(jnp.bfloat16)


def gather_split(rows, n_split):
    if n_split == 4:
        cross = lax.ppermute(rows, "split", [(0, 2), (1, 3), (2, 0), (3, 1)])
        pair = [(0, 1), (1, 0), (2, 3), (3, 2)]
        return [cross, lax.ppermute(rows, "split", pair), lax.ppermute(cross, "split", pair)]
    return [
        lax.ppermute(rows, "split", [(i, (i + d) % n_split) for i in range(n_split)])
        for d in range(1, n_split)
    ]


def unpack(buf, emb_w, n_all):
    emb = buf[:, :emb_w]
    lab = buf[:, emb_w].astype(jnp.float32)
    digits = [buf[:, emb_w + i].astype(jnp.float32) for i in (1, 2, 3)]
    return emb, lab, (digits[0] * n_all + digits[1] * 256.0) + digits[2]


def local(states, weight, cluster_id, block, order):
    n_doc = states.shape[0]
    n_grp = lax.axis_size("grp")
    n_split = lax.axis_size("split")
    n_dev = n_grp * n_split
    n_all = n_doc * n_dev
    cap = n_split * max(2, 2 * n_doc // n_dev)
    n_slot = n_grp * cap
    owner_of = cluster_id // CL_GRP
    onehot = (owner_of[:, None] == jnp.arange(n_grp, dtype=jnp.int32)[None, :]).astype(jnp.bfloat16)
    lower = (jnp.arange(n_doc)[:, None] > jnp.arange(n_doc)[None, :]).astype(jnp.bfloat16)
    before = jnp.dot(lower, onehot, preferred_element_type=jnp.float32)
    slot = jnp.sum(before * onehot.astype(jnp.float32), axis=1).astype(jnp.int32)
    place = owner_of * cap + slot

    embeds = embed_rows(states, weight)
    emb_w = embeds.shape[1]
    half = emb_w // 2
    label = (cluster_id - owner_of * CL_GRP + 1).astype(jnp.float32)
    meta_cols = jnp.stack(
        [label, block.astype(jnp.float32), (order // 256).astype(jnp.float32),
         (order % 256).astype(jnp.float32)],
        axis=1,
    )
    meta = jnp.concatenate(
        [meta_cols, jnp.zeros((n_doc, META - meta_cols.shape[1]), jnp.float32)], axis=1
    ).astype(jnp.bfloat16)
    pick = place[None, :] == jnp.arange(n_slot, dtype=jnp.int32)[:, None]

    def route(rows):
        send = jnp.dot(pick.astype(jnp.bfloat16), rows, preferred_element_type=jnp.float32)
        send = send.astype(jnp.bfloat16).reshape(n_grp, cap, -1)
        got = lax.all_to_all(send, "grp", split_axis=0, concat_axis=0, tiled=True)
        return got.reshape(n_slot, -1)

    if n_split == 4:
        half = emb_w - 3 * emb_w // 8
        cross = [(0, 2), (2, 0), (1, 3), (3, 1)]
        pair = [(0, 1), (1, 0), (2, 3), (3, 2)]
        raw_b = embeds[:, half:]
        par_b = lax.ppermute(raw_b, "split", cross)
        par_place = lax.ppermute(place, "split", cross)
        got_a = route(jnp.concatenate([embeds[:, :half], meta], axis=1))
        q_emb, q_lab, q_ord = unpack(got_a, half, n_all)
        keys_a = gather_split(q_emb, n_split)
        keys_m = gather_split(jnp.stack([q_lab, q_ord]), n_split)
        pick_par = par_place[None, :] == jnp.arange(n_slot, dtype=jnp.int32)[:, None]
        send_own = jnp.dot(pick.astype(jnp.bfloat16), raw_b, preferred_element_type=jnp.float32)
        send_par = jnp.dot(pick_par.astype(jnp.bfloat16), par_b, preferred_element_type=jnp.float32)
        send = jnp.concatenate(
            [send_own.reshape(n_grp, cap, -1), send_par.reshape(n_grp, cap, -1)], axis=1
        ).astype(jnp.bfloat16)
        got = lax.all_to_all(send, "grp", split_axis=0, concat_axis=0, tiled=True)
        got_b = got[:, :cap].reshape(n_slot, -1)
        cross_b = got[:, cap:].reshape(n_slot, -1)
        keys_b = [cross_b, lax.ppermute(got_b, "split", pair), lax.ppermute(cross_b, "split", pair)]
    else:
        half = emb_w // 2
        got_a = route(jnp.concatenate([embeds[:, :half], meta], axis=1))
        q_emb, q_lab, q_ord = unpack(got_a, half, n_all)
        keys_a = gather_split(q_emb, n_split)
        keys_m = gather_split(jnp.stack([q_lab, q_ord]), n_split)
        got_b = route(embeds[:, half:])
        keys_b = gather_split(got_b, n_split)

    def part(k_a, hits):
        s = jnp.einsum("qe,ke->qk", q_emb, k_a, preferred_element_type=jnp.float32)
        return jnp.where(hits, s, -jnp.inf)

    parts = [part(q_emb, (q_lab[:, None] == q_lab[None, :]) & (q_lab[None, :] > 0) & (q_ord[None, :] < q_ord[:, None]))]
    for k_a, k_m in zip(keys_a, keys_m):
        k_lab, k_ord = k_m[0], k_m[1]
        parts.append(part(k_a, (q_lab[:, None] == k_lab[None, :]) & (k_lab[None, :] > 0) & (k_ord[None, :] < q_ord[:, None])))
    best = jnp.full((n_slot,), -1.0, jnp.float32)
    for masked, k_b in zip(parts, [got_b] + list(keys_b)):
        s = masked + jnp.einsum("qe,ke->qk", got_b, k_b, preferred_element_type=jnp.float32)
        best = jnp.maximum(best, jnp.max(s, axis=1))

    returned = lax.all_to_all(
        best.reshape(n_grp, cap), "grp", split_axis=0, concat_axis=0, tiled=True
    ).reshape(n_slot)
    return jnp.max(jnp.where(pick, returned[:, None], -jnp.inf), axis=0)


def solution(mesh):
    in_specs = (
        P(("grp", "split"), None),
        P(),
        P(("grp", "split")),
        P(("grp", "split")),
        P(("grp", "split")),
    )
    out_specs = P(("grp", "split"))
    return jax.shard_map(local, mesh=mesh, in_specs=in_specs, out_specs=out_specs, check_vma=False)
```

```python
import jax
import jax.numpy as jnp
from jax import lax
from jax.sharding import PartitionSpec as P
from jax.experimental import pallas as pl

CL_GRP = 4


EPS = 1e-06
META = 128


def embed_rows(rows, weight):
    proj = jnp.einsum("...h,he->...e", rows, weight, preferred_element_type=jnp.float32)
    scale = lax.rsqrt(jnp.sum(proj * proj, axis=-1, keepdims=True) + EPS)
    return (proj * scale).astype(jnp.bfloat16)


def _block_max_kernel(qa_ref, qb_ref, ka_ref, kb_ref, qm_ref, km_ref, o_ref):
    nt = (((1,), (1,)), ((), ()))
    s = lax.dot_general(qa_ref[...], ka_ref[...], nt, preferred_element_type=jnp.float32)
    s = s + lax.dot_general(qb_ref[...], kb_ref[...], nt, preferred_element_type=jnp.float32)
    q_lab, q_ord = qm_ref[:, 0:1], qm_ref[:, 1:2]
    k_lab, k_ord = km_ref[0:1, :], km_ref[1:2, :]
    hits = (q_lab == k_lab) & (k_lab > 0) & (k_ord < q_ord)
    o_ref[...] = jnp.max(jnp.where(hits, s, jnp.float32(-1.0)), axis=1, keepdims=True)


def block_max(qa, qb, ka, kb, qm, km):
    n_q, n_k = qa.shape[0], ka.shape[0]
    tq = 256 if n_q % 256 == 0 else n_q
    wa, wb = qa.shape[1], qb.shape[1]
    cost = pl.CostEstimate(
        flops=2 * n_q * n_k * (wa + wb),
        bytes_accessed=2 * (n_q + n_k) * (wa + wb) + 4 * n_q * n_k // 64,
        transcendentals=0,
    )
    out = pl.pallas_call(
        _block_max_kernel,
        out_shape=jax.ShapeDtypeStruct((n_q, 1), jnp.float32),
        grid=(n_q // tq,),
        in_specs=[
            pl.BlockSpec((tq, wa), lambda i: (i, 0)),
            pl.BlockSpec((tq, wb), lambda i: (i, 0)),
            pl.BlockSpec((n_k, wa), lambda i: (0, 0)),
            pl.BlockSpec((n_k, wb), lambda i: (0, 0)),
            pl.BlockSpec((tq, qm.shape[1]), lambda i: (i, 0)),
            pl.BlockSpec((km.shape[0], n_k), lambda i: (0, 0)),
        ],
        out_specs=pl.BlockSpec((tq, 1), lambda i: (i, 0)),
        cost_estimate=cost,
    )(qa, qb, ka, kb, qm, km)
    return out[:, 0]


def gather_split(rows, n_split):
    if n_split == 4:
        cross = lax.ppermute(rows, "split", [(0, 2), (1, 3), (2, 0), (3, 1)])
        pair = [(0, 1), (1, 0), (2, 3), (3, 2)]
        return [cross, lax.ppermute(rows, "split", pair), lax.ppermute(cross, "split", pair)]
    return [
        lax.ppermute(rows, "split", [(i, (i + d) % n_split) for i in range(n_split)])
        for d in range(1, n_split)
    ]


def unpack(buf, emb_w, n_all):
    emb = buf[:, :emb_w]
    lab = buf[:, emb_w].astype(jnp.float32)
    digits = [buf[:, emb_w + i].astype(jnp.float32) for i in (1, 2, 3)]
    return emb, lab, (digits[0] * n_all + digits[1] * 256.0) + digits[2]


def local(states, weight, cluster_id, block, order):
    n_doc = states.shape[0]
    n_grp = lax.axis_size("grp")
    n_split = lax.axis_size("split")
    n_dev = n_grp * n_split
    n_all = n_doc * n_dev
    cap = n_split * max(2, 2 * n_doc // n_dev)
    n_slot = n_grp * cap
    owner_of = cluster_id // CL_GRP
    onehot = (owner_of[:, None] == jnp.arange(n_grp, dtype=jnp.int32)[None, :]).astype(jnp.bfloat16)
    lower = (jnp.arange(n_doc)[:, None] > jnp.arange(n_doc)[None, :]).astype(jnp.bfloat16)
    before = jnp.dot(lower, onehot, preferred_element_type=jnp.float32)
    slot = jnp.sum(before * onehot.astype(jnp.float32), axis=1).astype(jnp.int32)
    place = owner_of * cap + slot

    embeds = embed_rows(states, weight)
    emb_w = embeds.shape[1]
    half = emb_w // 2
    label = (cluster_id - owner_of * CL_GRP + 1).astype(jnp.float32)
    meta_cols = jnp.stack(
        [label, block.astype(jnp.float32), (order // 256).astype(jnp.float32),
         (order % 256).astype(jnp.float32)],
        axis=1,
    )
    meta = jnp.concatenate(
        [meta_cols, jnp.zeros((n_doc, META - meta_cols.shape[1]), jnp.float32)], axis=1
    ).astype(jnp.bfloat16)
    pick = place[None, :] == jnp.arange(n_slot, dtype=jnp.int32)[:, None]

    def route(rows):
        send = jnp.dot(pick.astype(jnp.bfloat16), rows, preferred_element_type=jnp.float32)
        send = send.astype(jnp.bfloat16).reshape(n_grp, cap, -1)
        got = lax.all_to_all(send, "grp", split_axis=0, concat_axis=0, tiled=True)
        return got.reshape(n_slot, -1)

    if n_split == 4:
        half = emb_w - 3 * emb_w // 8
        cross = [(0, 2), (2, 0), (1, 3), (3, 1)]
        pair = [(0, 1), (1, 0), (2, 3), (3, 2)]
        raw_b = embeds[:, half:]
        par_b = lax.ppermute(raw_b, "split", cross)
        par_place = lax.ppermute(place, "split", cross)
        got_a = route(jnp.concatenate([embeds[:, :half], meta], axis=1))
        q_emb, q_lab, q_ord = unpack(got_a, half, n_all)
        keys_a = gather_split(q_emb, n_split)
        keys_m = gather_split(jnp.stack([q_lab, q_ord]), n_split)
        pick_par = par_place[None, :] == jnp.arange(n_slot, dtype=jnp.int32)[:, None]
        send_own = jnp.dot(pick.astype(jnp.bfloat16), raw_b, preferred_element_type=jnp.float32)
        send_par = jnp.dot(pick_par.astype(jnp.bfloat16), par_b, preferred_element_type=jnp.float32)
        send = jnp.concatenate(
            [send_own.reshape(n_grp, cap, -1), send_par.reshape(n_grp, cap, -1)], axis=1
        ).astype(jnp.bfloat16)
        got = lax.all_to_all(send, "grp", split_axis=0, concat_axis=0, tiled=True)
        got_b = got[:, :cap].reshape(n_slot, -1)
        cross_b = got[:, cap:].reshape(n_slot, -1)
        keys_b = [cross_b, lax.ppermute(got_b, "split", pair), lax.ppermute(cross_b, "split", pair)]
    else:
        half = emb_w // 2
        got_a = route(jnp.concatenate([embeds[:, :half], meta], axis=1))
        q_emb, q_lab, q_ord = unpack(got_a, half, n_all)
        keys_a = gather_split(q_emb, n_split)
        keys_m = gather_split(jnp.stack([q_lab, q_ord]), n_split)
        got_b = route(embeds[:, half:])
        keys_b = gather_split(got_b, n_split)

    own_m = jnp.stack([q_lab, q_ord])
    pad_m = jnp.zeros((6, n_slot), jnp.float32)
    qm = jnp.concatenate([own_m, pad_m], axis=0).T
    best = jnp.full((n_slot,), -1.0, jnp.float32)
    for k_a, k_b, k_m in zip([q_emb] + list(keys_a), [got_b] + list(keys_b), [own_m] + list(keys_m)):
        km = jnp.concatenate([k_m, pad_m], axis=0)
        best = jnp.maximum(best, block_max(q_emb, got_b, k_a, k_b, qm, km))

    returned = lax.all_to_all(
        best.reshape(n_grp, cap), "grp", split_axis=0, concat_axis=0, tiled=True
    ).reshape(n_slot)
    return jnp.max(jnp.where(pick, returned[:, None], -jnp.inf), axis=0)


def solution(mesh):
    in_specs = (
        P(("grp", "split"), None),
        P(),
        P(("grp", "split")),
        P(("grp", "split")),
        P(("grp", "split")),
    )
    out_specs = P(("grp", "split"))
    return jax.shard_map(local, mesh=mesh, in_specs=in_specs, out_specs=out_specs, check_vma=False)
```

```python
import jax
import jax.numpy as jnp
from jax import lax
from jax.sharding import PartitionSpec as P

CL_GRP = 4


EPS = 1e-06
META = 128


def embed_rows(rows, weight):
    proj = jnp.einsum("...h,he->...e", rows, weight, preferred_element_type=jnp.float32)
    scale = lax.rsqrt(jnp.sum(proj * proj, axis=-1, keepdims=True) + EPS)
    return (proj * scale).astype(jnp.bfloat16)


def gather_split(rows, n_split):
    if n_split == 4:
        cross = lax.ppermute(rows, "split", [(0, 2), (1, 3), (2, 0), (3, 1)])
        pair = [(0, 1), (1, 0), (2, 3), (3, 2)]
        return [cross, lax.ppermute(rows, "split", pair), lax.ppermute(cross, "split", pair)]
    return [
        lax.ppermute(rows, "split", [(i, (i + d) % n_split) for i in range(n_split)])
        for d in range(1, n_split)
    ]


def unpack(buf, emb_w, n_all):
    emb = buf[:, :emb_w]
    lab = buf[:, emb_w].astype(jnp.float32)
    digits = [buf[:, emb_w + i].astype(jnp.float32) for i in (1, 2, 3)]
    return emb, lab, (digits[0] * n_all + digits[1] * 256.0) + digits[2]


def local(states, weight, cluster_id, block, order):
    n_doc = states.shape[0]
    n_grp = lax.axis_size("grp")
    n_split = lax.axis_size("split")
    n_dev = n_grp * n_split
    n_all = n_doc * n_dev
    cap = n_split * max(2, 2 * n_doc // n_dev)
    n_slot = n_grp * cap
    owner_of = cluster_id // CL_GRP
    onehot = (owner_of[:, None] == jnp.arange(n_grp, dtype=jnp.int32)[None, :]).astype(jnp.bfloat16)
    lower = (jnp.arange(n_doc)[:, None] > jnp.arange(n_doc)[None, :]).astype(jnp.bfloat16)
    before = jnp.dot(lower, onehot, preferred_element_type=jnp.float32)
    slot = jnp.sum(before * onehot.astype(jnp.float32), axis=1).astype(jnp.int32)
    place = owner_of * cap + slot

    embeds = embed_rows(states, weight)
    emb_w = embeds.shape[1]
    half = emb_w // 2
    label = (cluster_id - owner_of * CL_GRP + 1).astype(jnp.float32)
    meta_cols = jnp.stack(
        [label, block.astype(jnp.float32), (order // 256).astype(jnp.float32),
         (order % 256).astype(jnp.float32)],
        axis=1,
    )
    meta = jnp.concatenate(
        [meta_cols, jnp.zeros((n_doc, META - meta_cols.shape[1]), jnp.float32)], axis=1
    ).astype(jnp.bfloat16)
    pick = place[None, :] == jnp.arange(n_slot, dtype=jnp.int32)[:, None]

    def route(rows):
        send = jnp.dot(pick.astype(jnp.bfloat16), rows, preferred_element_type=jnp.float32)
        send = send.astype(jnp.bfloat16).reshape(n_grp, cap, -1)
        got = lax.all_to_all(send, "grp", split_axis=0, concat_axis=0, tiled=True)
        return got.reshape(n_slot, -1)

    if n_split == 4:
        half = emb_w - 3 * emb_w // 8
        cross = [(0, 2), (2, 0), (1, 3), (3, 1)]
        pair = [(0, 1), (1, 0), (2, 3), (3, 2)]
        raw_b = embeds[:, half:]
        par_b = lax.ppermute(raw_b, "split", cross)
        par_place = lax.ppermute(place, "split", cross)
        got_a = route(jnp.concatenate([embeds[:, :half], meta], axis=1))
        q_emb, q_lab, q_ord = unpack(got_a, half, n_all)
        keys_a = gather_split(q_emb, n_split)
        keys_m = gather_split(jnp.stack([q_lab, q_ord]), n_split)
        pick_par = par_place[None, :] == jnp.arange(n_slot, dtype=jnp.int32)[:, None]
        send_own = jnp.dot(pick.astype(jnp.bfloat16), raw_b, preferred_element_type=jnp.float32)
        send_par = jnp.dot(pick_par.astype(jnp.bfloat16), par_b, preferred_element_type=jnp.float32)
        send = jnp.concatenate(
            [send_own.reshape(n_grp, cap, -1), send_par.reshape(n_grp, cap, -1)], axis=1
        ).astype(jnp.bfloat16)
        got = lax.all_to_all(send, "grp", split_axis=0, concat_axis=0, tiled=True)
        got_b = got[:, :cap].reshape(n_slot, -1)
        cross_b = got[:, cap:].reshape(n_slot, -1)
        keys_b = [cross_b, lax.ppermute(got_b, "split", pair), lax.ppermute(cross_b, "split", pair)]
    else:
        half = emb_w // 2
        got_a = route(jnp.concatenate([embeds[:, :half], meta], axis=1))
        q_emb, q_lab, q_ord = unpack(got_a, half, n_all)
        keys_a = gather_split(q_emb, n_split)
        keys_m = gather_split(jnp.stack([q_lab, q_ord]), n_split)
        got_b = route(embeds[:, half:])
        keys_b = gather_split(got_b, n_split)

    def part(q, k, hits):
        s = jnp.einsum("qe,ke->qk", q, k, preferred_element_type=jnp.float32)
        return jnp.where(hits, s, -jnp.inf)

    own_hits = (q_lab[:, None] == q_lab[None, :]) & (q_lab[None, :] > 0) & (q_ord[None, :] < q_ord[:, None])
    parts = [lax.optimization_barrier(part(q_emb, q_emb, own_hits))]
    for k_a, k_m in zip(keys_a, keys_m):
        k_lab, k_ord = k_m[0], k_m[1]
        hits = (q_lab[:, None] == k_lab[None, :]) & (k_lab[None, :] > 0) & (k_ord[None, :] < q_ord[:, None])
        parts.append(lax.optimization_barrier(part(q_emb, k_a, hits)))
    best = jnp.full((n_slot,), -1.0, jnp.float32)
    for masked, k_b in zip(parts, [got_b] + list(keys_b)):
        second = lax.optimization_barrier(
            jnp.einsum("qe,ke->qk", got_b, k_b, preferred_element_type=jnp.float32)
        )
        best = jnp.maximum(best, jnp.max(masked + second, axis=1))

    returned = lax.all_to_all(
        best.reshape(n_grp, cap), "grp", split_axis=0, concat_axis=0, tiled=True
    ).reshape(n_slot)
    return jnp.max(jnp.where(pick, returned[:, None], -jnp.inf), axis=0)


def solution(mesh):
    in_specs = (
        P(("grp", "split"), None),
        P(),
        P(("grp", "split")),
        P(("grp", "split")),
        P(("grp", "split")),
    )
    out_specs = P(("grp", "split"))
    return jax.shard_map(local, mesh=mesh, in_specs=in_specs, out_specs=out_specs, check_vma=False)
```

```python
import jax
import jax.numpy as jnp
from jax import lax
from jax.sharding import PartitionSpec as P

CL_GRP = 4


EPS = 1e-06
META = 128


def embed_rows(rows, weight):
    proj = jnp.einsum("...h,he->...e", rows, weight, preferred_element_type=jnp.float32)
    scale = lax.rsqrt(jnp.sum(proj * proj, axis=-1, keepdims=True) + EPS)
    return (proj * scale).astype(jnp.bfloat16)


def gather_split(rows, n_split):
    if n_split == 4:
        cross = lax.ppermute(rows, "split", [(0, 2), (1, 3), (2, 0), (3, 1)])
        pair = [(0, 1), (1, 0), (2, 3), (3, 2)]
        return [cross, lax.ppermute(rows, "split", pair), lax.ppermute(cross, "split", pair)]
    return [
        lax.ppermute(rows, "split", [(i, (i + d) % n_split) for i in range(n_split)])
        for d in range(1, n_split)
    ]


def unpack(buf, emb_w, n_all):
    emb = buf[:, :emb_w]
    lab = buf[:, emb_w].astype(jnp.float32)
    digits = [buf[:, emb_w + i].astype(jnp.float32) for i in (1, 2, 3)]
    return emb, lab, (digits[0] * n_all + digits[1] * 256.0) + digits[2]


def local(states, weight, cluster_id, block, order):
    n_doc = states.shape[0]
    n_grp = lax.axis_size("grp")
    n_split = lax.axis_size("split")
    n_dev = n_grp * n_split
    n_all = n_doc * n_dev
    cap = n_split * max(2, 2 * n_doc // n_dev)
    n_slot = n_grp * cap
    owner_of = cluster_id // CL_GRP
    onehot = (owner_of[:, None] == jnp.arange(n_grp, dtype=jnp.int32)[None, :]).astype(jnp.bfloat16)
    lower = (jnp.arange(n_doc)[:, None] > jnp.arange(n_doc)[None, :]).astype(jnp.bfloat16)
    before = jnp.dot(lower, onehot, preferred_element_type=jnp.float32)
    slot = jnp.sum(before * onehot.astype(jnp.float32), axis=1).astype(jnp.int32)
    place = owner_of * cap + slot

    embeds = embed_rows(states, weight)
    emb_w = embeds.shape[1]
    half = emb_w // 2
    label = (cluster_id - owner_of * CL_GRP + 1).astype(jnp.float32)
    meta_cols = jnp.stack(
        [label, block.astype(jnp.float32), (order // 256).astype(jnp.float32),
         (order % 256).astype(jnp.float32)],
        axis=1,
    )
    meta = jnp.concatenate(
        [meta_cols, jnp.zeros((n_doc, META - meta_cols.shape[1]), jnp.float32)], axis=1
    ).astype(jnp.bfloat16)
    pick = place[None, :] == jnp.arange(n_slot, dtype=jnp.int32)[:, None]

    def route(rows):
        send = jnp.dot(pick.astype(jnp.bfloat16), rows, preferred_element_type=jnp.float32)
        send = send.astype(jnp.bfloat16).reshape(n_grp, cap, -1)
        got = lax.all_to_all(send, "grp", split_axis=0, concat_axis=0, tiled=True)
        return got.reshape(n_slot, -1)

    if n_split == 4:
        half = emb_w // 2
        cross = [(0, 2), (2, 0), (1, 3), (3, 1)]
        pair = [(0, 1), (1, 0), (2, 3), (3, 2)]
        raw_b = embeds[:, half:]
        par_b = lax.ppermute(raw_b, "split", cross)
        par_place = lax.ppermute(place, "split", cross)
        got_a = route(jnp.concatenate([embeds[:, :half], meta], axis=1))
        q_emb, q_lab, q_ord = unpack(got_a, half, n_all)
        keys_a = gather_split(q_emb, n_split)
        keys_m = gather_split(jnp.stack([q_lab, q_ord]), n_split)
        pick_par = par_place[None, :] == jnp.arange(n_slot, dtype=jnp.int32)[:, None]
        send_own = jnp.dot(pick.astype(jnp.bfloat16), raw_b, preferred_element_type=jnp.float32)
        send_par = jnp.dot(pick_par.astype(jnp.bfloat16), par_b, preferred_element_type=jnp.float32)
        send = jnp.concatenate(
            [send_own.reshape(n_grp, cap, -1), send_par.reshape(n_grp, cap, -1)], axis=1
        ).astype(jnp.bfloat16)
        got = lax.all_to_all(send, "grp", split_axis=0, concat_axis=0, tiled=True)
        got_b = got[:, :cap].reshape(n_slot, -1)
        cross_b = got[:, cap:].reshape(n_slot, -1)
        keys_b = [cross_b, lax.ppermute(got_b, "split", pair), lax.ppermute(cross_b, "split", pair)]
    else:
        half = emb_w // 2
        got_a = route(jnp.concatenate([embeds[:, :half], meta], axis=1))
        q_emb, q_lab, q_ord = unpack(got_a, half, n_all)
        keys_a = gather_split(q_emb, n_split)
        keys_m = gather_split(jnp.stack([q_lab, q_ord]), n_split)
        got_b = route(embeds[:, half:])
        keys_b = gather_split(got_b, n_split)

    def part(q, k, hits):
        s = jnp.einsum("qe,ke->qk", q, k, preferred_element_type=jnp.float32)
        return jnp.where(hits, s, -jnp.inf)

    q_base = q_lab * 1048576.0
    q_code = q_base + q_ord

    def hits_of(k_lab, k_ord):
        k_code = k_lab * 1048576.0 + k_ord
        return (k_code[None, :] >= q_base[:, None]) & (k_code[None, :] < q_code[:, None])

    parts = [lax.optimization_barrier(part(q_emb, q_emb, hits_of(q_lab, q_ord)))]
    for k_a, k_m in zip(keys_a, keys_m):
        parts.append(lax.optimization_barrier(part(q_emb, k_a, hits_of(k_m[0], k_m[1]))))
    best = jnp.full((n_slot,), -1.0, jnp.float32)
    for masked, k_b in zip(parts, [got_b] + list(keys_b)):
        second = lax.optimization_barrier(
            jnp.einsum("qe,ke->qk", got_b, k_b, preferred_element_type=jnp.float32)
        )
        best = jnp.maximum(best, jnp.max(masked + second, axis=1))

    returned = lax.all_to_all(
        best.reshape(n_grp, cap), "grp", split_axis=0, concat_axis=0, tiled=True
    ).reshape(n_slot)
    return jnp.max(jnp.where(pick, returned[:, None], -jnp.inf), axis=0)


def solution(mesh):
    in_specs = (
        P(("grp", "split"), None),
        P(),
        P(("grp", "split")),
        P(("grp", "split")),
        P(("grp", "split")),
    )
    out_specs = P(("grp", "split"))
    return jax.shard_map(local, mesh=mesh, in_specs=in_specs, out_specs=out_specs, check_vma=False)
```

```python
import jax
import jax.numpy as jnp
from jax import lax
from jax.sharding import PartitionSpec as P

CL_GRP = 4


EPS = 1e-06
META = 128


def embed_rows(rows, weight):
    proj = jnp.einsum("...h,he->...e", rows, weight, preferred_element_type=jnp.float32)
    scale = lax.rsqrt(jnp.sum(proj * proj, axis=-1, keepdims=True) + EPS)
    return (proj * scale).astype(jnp.bfloat16)


def gather_split(rows, n_split):
    if n_split == 4:
        cross = lax.ppermute(rows, "split", [(0, 2), (1, 3), (2, 0), (3, 1)])
        pair = [(0, 1), (1, 0), (2, 3), (3, 2)]
        return [cross, lax.ppermute(rows, "split", pair), lax.ppermute(cross, "split", pair)]
    return [
        lax.ppermute(rows, "split", [(i, (i + d) % n_split) for i in range(n_split)])
        for d in range(1, n_split)
    ]


def unpack(buf, emb_w, n_all):
    emb = buf[:, :emb_w]
    lab = buf[:, emb_w].astype(jnp.float32)
    digits = [buf[:, emb_w + i].astype(jnp.float32) for i in (1, 2, 3)]
    return emb, lab, (digits[0] * n_all + digits[1] * 256.0) + digits[2]


def local(states, weight, cluster_id, block, order):
    n_doc = states.shape[0]
    n_grp = lax.axis_size("grp")
    n_split = lax.axis_size("split")
    n_dev = n_grp * n_split
    n_all = n_doc * n_dev
    cap = n_split * max(2, 2 * n_doc // n_dev)
    n_slot = n_grp * cap
    owner_of = cluster_id // CL_GRP
    onehot = (owner_of[:, None] == jnp.arange(n_grp, dtype=jnp.int32)[None, :]).astype(jnp.bfloat16)
    lower = (jnp.arange(n_doc)[:, None] > jnp.arange(n_doc)[None, :]).astype(jnp.bfloat16)
    before = jnp.dot(lower, onehot, preferred_element_type=jnp.float32)
    slot = jnp.sum(before * onehot.astype(jnp.float32), axis=1).astype(jnp.int32)
    place = owner_of * cap + slot

    embeds = embed_rows(states, weight)
    emb_w = embeds.shape[1]
    half = emb_w // 2
    label = (cluster_id - owner_of * CL_GRP + 1).astype(jnp.float32)
    meta_cols = jnp.stack(
        [label, block.astype(jnp.float32), (order // 256).astype(jnp.float32),
         (order % 256).astype(jnp.float32)],
        axis=1,
    )
    meta = jnp.concatenate(
        [meta_cols, jnp.zeros((n_doc, META - meta_cols.shape[1]), jnp.float32)], axis=1
    ).astype(jnp.bfloat16)
    pick = place[None, :] == jnp.arange(n_slot, dtype=jnp.int32)[:, None]

    def route(rows):
        send = jnp.dot(pick.astype(jnp.bfloat16), rows, preferred_element_type=jnp.float32)
        send = send.astype(jnp.bfloat16).reshape(n_grp, cap, -1)
        got = lax.all_to_all(send, "grp", split_axis=0, concat_axis=0, tiled=True)
        return got.reshape(n_slot, -1)

    if n_split == 4:
        half = emb_w - 3 * emb_w // 8
        cross = [(0, 2), (2, 0), (1, 3), (3, 1)]
        pair = [(0, 1), (1, 0), (2, 3), (3, 2)]
        raw_b = embeds[:, half:]
        par_b = lax.ppermute(raw_b, "split", cross)
        par_place = lax.ppermute(place, "split", cross)
        col = jnp.arange(half + META, dtype=jnp.int32)[None, :]
        rows_a = jnp.where(
            col < half,
            jnp.pad(embeds[:, :half], ((0, 0), (0, META))),
            jnp.pad(meta, ((0, 0), (half, 0))),
        )
        got_a = route(rows_a)
        q_emb, q_lab, q_ord = unpack(got_a, half, n_all)
        keys_a = gather_split(q_emb, n_split)
        keys_m = gather_split(jnp.stack([q_lab, q_ord]), n_split)
        pick_par = par_place[None, :] == jnp.arange(n_slot, dtype=jnp.int32)[:, None]
        send_own = jnp.dot(pick.astype(jnp.bfloat16), raw_b, preferred_element_type=jnp.float32)
        send_par = jnp.dot(pick_par.astype(jnp.bfloat16), par_b, preferred_element_type=jnp.float32)
        send = jnp.concatenate(
            [send_own.reshape(n_grp, cap, -1), send_par.reshape(n_grp, cap, -1)], axis=1
        ).astype(jnp.bfloat16)
        got = lax.all_to_all(send, "grp", split_axis=0, concat_axis=0, tiled=True)
        got_b = got[:, :cap].reshape(n_slot, -1)
        cross_b = got[:, cap:].reshape(n_slot, -1)
        keys_b = [cross_b, lax.ppermute(got_b, "split", pair), lax.ppermute(cross_b, "split", pair)]
    else:
        half = emb_w // 2
        got_a = route(jnp.concatenate([embeds[:, :half], meta], axis=1))
        q_emb, q_lab, q_ord = unpack(got_a, half, n_all)
        keys_a = gather_split(q_emb, n_split)
        keys_m = gather_split(jnp.stack([q_lab, q_ord]), n_split)
        got_b = route(embeds[:, half:])
        keys_b = gather_split(got_b, n_split)

    def dots(k_a, k_b):
        s = jnp.einsum("qe,ke->qk", q_emb, k_a, preferred_element_type=jnp.float32)
        return s + jnp.einsum("qe,ke->qk", got_b, k_b, preferred_element_type=jnp.float32)

    scores = dots(q_emb, got_b)
    hits = (q_lab[:, None] == q_lab[None, :]) & (q_lab[None, :] > 0) & (q_ord[None, :] < q_ord[:, None])
    best = jnp.max(jnp.where(hits, scores, jnp.float32(-1.0)), axis=1)
    for k_a, k_b, k_m in zip(keys_a, keys_b, keys_m):
        k_lab, k_ord = k_m[0], k_m[1]
        scores = dots(k_a, k_b)
        hits = (q_lab[:, None] == k_lab[None, :]) & (k_lab[None, :] > 0) & (k_ord[None, :] < q_ord[:, None])
        best = jnp.maximum(best, jnp.max(jnp.where(hits, scores, jnp.float32(-1.0)), axis=1))

    returned = lax.all_to_all(
        best.reshape(n_grp, cap), "grp", split_axis=0, concat_axis=0, tiled=True
    ).reshape(n_slot)
    return jnp.max(jnp.where(pick, returned[:, None], -jnp.inf), axis=0)


def solution(mesh):
    in_specs = (
        P(("grp", "split"), None),
        P(),
        P(("grp", "split")),
        P(("grp", "split")),
        P(("grp", "split")),
    )
    out_specs = P(("grp", "split"))
    return jax.shard_map(local, mesh=mesh, in_specs=in_specs, out_specs=out_specs, check_vma=False)
```

```python
import jax
import jax.numpy as jnp
from jax import lax
from jax.sharding import PartitionSpec as P

CL_GRP = 4


EPS = 1e-06
META = 128


def embed_rows(rows, weight):
    proj = jnp.einsum("...h,he->...e", rows, weight, preferred_element_type=jnp.float32)
    scale = lax.rsqrt(jnp.sum(proj * proj, axis=-1, keepdims=True) + EPS)
    return (proj * scale).astype(jnp.bfloat16)


def gather_split(rows, n_split):
    if n_split == 4:
        cross = lax.ppermute(rows, "split", [(0, 2), (1, 3), (2, 0), (3, 1)])
        pair = [(0, 1), (1, 0), (2, 3), (3, 2)]
        return [cross, lax.ppermute(rows, "split", pair), lax.ppermute(cross, "split", pair)]
    return [
        lax.ppermute(rows, "split", [(i, (i + d) % n_split) for i in range(n_split)])
        for d in range(1, n_split)
    ]


def unpack(buf, emb_w, n_all):
    emb = buf[:, :emb_w]
    lab = buf[:, emb_w].astype(jnp.float32)
    digits = [buf[:, emb_w + i].astype(jnp.float32) for i in (1, 2, 3)]
    return emb, lab, (digits[0] * n_all + digits[1] * 256.0) + digits[2]


def local(states, weight, cluster_id, block, order):
    n_doc = states.shape[0]
    n_grp = lax.axis_size("grp")
    n_split = lax.axis_size("split")
    n_dev = n_grp * n_split
    n_all = n_doc * n_dev
    cap = n_split * max(2, 2 * n_doc // n_dev)
    n_slot = n_grp * cap
    owner_of = cluster_id // CL_GRP
    onehot = (owner_of[:, None] == jnp.arange(n_grp, dtype=jnp.int32)[None, :]).astype(jnp.bfloat16)
    lower = (jnp.arange(n_doc)[:, None] > jnp.arange(n_doc)[None, :]).astype(jnp.bfloat16)
    before = jnp.dot(lower, onehot, preferred_element_type=jnp.float32)
    slot = jnp.sum(before * onehot.astype(jnp.float32), axis=1).astype(jnp.int32)
    place = owner_of * cap + slot

    embeds = embed_rows(states, weight)
    emb_w = embeds.shape[1]
    half = emb_w // 2
    label = (cluster_id - owner_of * CL_GRP + 1).astype(jnp.float32)
    digits = [label, block.astype(jnp.float32), (order // 256).astype(jnp.float32), (order % 256).astype(jnp.float32)]
    mcol = jnp.arange(META, dtype=jnp.int32)[None, :]
    meta = jnp.zeros((n_doc, META), jnp.float32)
    for i, d in enumerate(digits):
        meta = jnp.where(mcol == i, d[:, None], meta)
    meta = meta.astype(jnp.bfloat16)
    pick = place[None, :] == jnp.arange(n_slot, dtype=jnp.int32)[:, None]

    def route(rows):
        send = jnp.dot(pick.astype(jnp.bfloat16), rows, preferred_element_type=jnp.float32)
        send = send.astype(jnp.bfloat16).reshape(n_grp, cap, -1)
        got = lax.all_to_all(send, "grp", split_axis=0, concat_axis=0, tiled=True)
        return got.reshape(n_slot, -1)

    if n_split == 4:
        half = emb_w - 3 * emb_w // 8
        cross = [(0, 2), (2, 0), (1, 3), (3, 1)]
        pair = [(0, 1), (1, 0), (2, 3), (3, 2)]
        raw_b = embeds[:, half:]
        par_b = lax.ppermute(raw_b, "split", cross)
        par_place = lax.ppermute(place, "split", cross)
        col = jnp.arange(half + META, dtype=jnp.int32)[None, :]
        rows_a = jnp.where(
            col < half,
            jnp.pad(embeds[:, :half], ((0, 0), (0, META))),
            jnp.pad(meta, ((0, 0), (half, 0))),
        )
        got_a = route(rows_a)
        q_emb, q_lab, q_ord = unpack(got_a, half, n_all)
        keys_a = gather_split(q_emb, n_split)
        keys_m = gather_split(jnp.stack([q_lab, q_ord]), n_split)
        pick_par = par_place[None, :] == jnp.arange(n_slot, dtype=jnp.int32)[:, None]
        send_own = jnp.dot(pick.astype(jnp.bfloat16), raw_b, preferred_element_type=jnp.float32)
        send_par = jnp.dot(pick_par.astype(jnp.bfloat16), par_b, preferred_element_type=jnp.float32)
        send = jnp.concatenate(
            [send_own.reshape(n_grp, cap, -1), send_par.reshape(n_grp, cap, -1)], axis=1
        ).astype(jnp.bfloat16)
        got = lax.all_to_all(send, "grp", split_axis=0, concat_axis=0, tiled=True)
        got_b = got[:, :cap].reshape(n_slot, -1)
        cross_b = got[:, cap:].reshape(n_slot, -1)
        keys_b = [cross_b, lax.ppermute(got_b, "split", pair), lax.ppermute(cross_b, "split", pair)]
    else:
        half = emb_w // 2
        got_a = route(jnp.concatenate([embeds[:, :half], meta], axis=1))
        q_emb, q_lab, q_ord = unpack(got_a, half, n_all)
        keys_a = gather_split(q_emb, n_split)
        keys_m = gather_split(jnp.stack([q_lab, q_ord]), n_split)
        got_b = route(embeds[:, half:])
        keys_b = gather_split(got_b, n_split)

    def dots(k_a, k_b):
        s = jnp.einsum("qe,ke->qk", q_emb, k_a, preferred_element_type=jnp.float32)
        return s + jnp.einsum("qe,ke->qk", got_b, k_b, preferred_element_type=jnp.float32)

    scores = dots(q_emb, got_b)
    hits = (q_lab[:, None] == q_lab[None, :]) & (q_lab[None, :] > 0) & (q_ord[None, :] < q_ord[:, None])
    best = jnp.max(jnp.where(hits, scores, jnp.float32(-1.0)), axis=1)
    for k_a, k_b, k_m in zip(keys_a, keys_b, keys_m):
        k_lab, k_ord = k_m[0], k_m[1]
        scores = dots(k_a, k_b)
        hits = (q_lab[:, None] == k_lab[None, :]) & (k_lab[None, :] > 0) & (k_ord[None, :] < q_ord[:, None])
        best = jnp.maximum(best, jnp.max(jnp.where(hits, scores, jnp.float32(-1.0)), axis=1))

    returned = lax.all_to_all(
        best.reshape(n_grp, cap), "grp", split_axis=0, concat_axis=0, tiled=True
    ).reshape(n_slot)
    return jnp.max(jnp.where(pick, returned[:, None], -jnp.inf), axis=0)


def solution(mesh):
    in_specs = (
        P(("grp", "split"), None),
        P(),
        P(("grp", "split")),
        P(("grp", "split")),
        P(("grp", "split")),
    )
    out_specs = P(("grp", "split"))
    return jax.shard_map(local, mesh=mesh, in_specs=in_specs, out_specs=out_specs, check_vma=False)
```

```python
import jax
import jax.numpy as jnp
from jax import lax
from jax.sharding import PartitionSpec as P

CL_GRP = 4


EPS = 1e-06
META = 128


def embed_rows(rows, weight):
    proj = jnp.einsum("...h,he->...e", rows, weight, preferred_element_type=jnp.float32)
    scale = lax.rsqrt(jnp.sum(proj * proj, axis=-1, keepdims=True) + EPS)
    return (proj * scale).astype(jnp.bfloat16)


def gather_split(rows, n_split):
    if n_split == 4:
        cross = lax.ppermute(rows, "split", [(0, 2), (1, 3), (2, 0), (3, 1)])
        pair = [(0, 1), (1, 0), (2, 3), (3, 2)]
        return [cross, lax.ppermute(rows, "split", pair), lax.ppermute(cross, "split", pair)]
    return [
        lax.ppermute(rows, "split", [(i, (i + d) % n_split) for i in range(n_split)])
        for d in range(1, n_split)
    ]


def unpack(buf, emb_w, n_all):
    emb = buf[:, :emb_w]
    lab = buf[:, emb_w].astype(jnp.float32)
    digits = [buf[:, emb_w + i].astype(jnp.float32) for i in (1, 2, 3)]
    return emb, lab, (digits[0] * n_all + digits[1] * 256.0) + digits[2]


def local(states, weight, cluster_id, block, order):
    n_doc = states.shape[0]
    n_grp = lax.axis_size("grp")
    n_split = lax.axis_size("split")
    n_dev = n_grp * n_split
    n_all = n_doc * n_dev
    cap = n_split * max(2, 2 * n_doc // n_dev)
    n_slot = n_grp * cap
    owner_of = cluster_id // CL_GRP
    onehot = (owner_of[:, None] == jnp.arange(n_grp, dtype=jnp.int32)[None, :]).astype(jnp.bfloat16)
    lower = (jnp.arange(n_doc)[:, None] > jnp.arange(n_doc)[None, :]).astype(jnp.bfloat16)
    before = jnp.dot(lower, onehot, preferred_element_type=jnp.float32)
    slot = jnp.sum(before * onehot.astype(jnp.float32), axis=1).astype(jnp.int32)
    place = owner_of * cap + slot

    embeds = embed_rows(states, weight)
    emb_w = embeds.shape[1]
    half = emb_w // 2
    label = (cluster_id - owner_of * CL_GRP + 1).astype(jnp.float32)
    digits = [label, block.astype(jnp.float32), (order // 256).astype(jnp.float32), (order % 256).astype(jnp.float32)]
    mcol = jnp.arange(META, dtype=jnp.int32)[None, :]
    meta = jnp.zeros((n_doc, META), jnp.float32)
    for i, d in enumerate(digits):
        meta = jnp.where(mcol == i, d[:, None], meta)
    meta = meta.astype(jnp.bfloat16)
    pick = place[None, :] == jnp.arange(n_slot, dtype=jnp.int32)[:, None]

    def route(rows):
        send = jnp.dot(pick.astype(jnp.bfloat16), rows, preferred_element_type=jnp.float32)
        send = send.astype(jnp.bfloat16).reshape(n_grp, cap, -1)
        got = lax.all_to_all(send, "grp", split_axis=0, concat_axis=0, tiled=True)
        return got.reshape(n_slot, -1)

    if n_split == 4:
        half = emb_w - 3 * emb_w // 8
        cross = [(0, 2), (2, 0), (1, 3), (3, 1)]
        pair = [(0, 1), (1, 0), (2, 3), (3, 2)]
        raw_b = embeds[:, half:]
        par_b = lax.ppermute(raw_b, "split", cross)
        par_place = lax.ppermute(place, "split", cross)
        col = jnp.arange(half + META, dtype=jnp.int32)[None, :]
        rows_a = jnp.where(
            col < half,
            jnp.pad(embeds[:, :half], ((0, 0), (0, META))),
            jnp.pad(meta, ((0, 0), (half, 0))),
        )
        got_a = route(rows_a)
        q_emb, q_lab, q_ord = unpack(got_a, half, n_all)
        keys_a = gather_split(q_emb, n_split)
        keys_m = gather_split(jnp.stack([q_lab, q_ord]), n_split)
        pick_par = par_place[None, :] == jnp.arange(n_slot, dtype=jnp.int32)[:, None]
        send_own = jnp.dot(pick.astype(jnp.bfloat16), raw_b, preferred_element_type=jnp.float32)
        send_par = jnp.dot(pick_par.astype(jnp.bfloat16), par_b, preferred_element_type=jnp.float32)
        send = jnp.concatenate(
            [send_own.reshape(n_grp, cap, -1), send_par.reshape(n_grp, cap, -1)], axis=1
        ).astype(jnp.bfloat16)
        got = lax.all_to_all(send, "grp", split_axis=0, concat_axis=0, tiled=True)
        got_b = got[:, :cap].reshape(n_slot, -1)
        cross_b = got[:, cap:].reshape(n_slot, -1)
        keys_b = [cross_b, lax.ppermute(got_b, "split", pair), lax.ppermute(cross_b, "split", pair)]
    else:
        half = emb_w // 2
        got_a = route(jnp.concatenate([embeds[:, :half], meta], axis=1))
        q_emb, q_lab, q_ord = unpack(got_a, half, n_all)
        keys_a = gather_split(q_emb, n_split)
        keys_m = gather_split(jnp.stack([q_lab, q_ord]), n_split)
        got_b = route(embeds[:, half:])
        keys_b = gather_split(got_b, n_split)

    def dots(k_a, k_b):
        s = jnp.einsum("qe,ke->qk", q_emb, k_a, preferred_element_type=jnp.float32)
        return s + jnp.einsum("qe,ke->qk", got_b, k_b, preferred_element_type=jnp.float32)

    scores = dots(q_emb, got_b)
    hits = (q_lab[:, None] == q_lab[None, :]) & (q_lab[None, :] > 0) & (q_ord[None, :] < q_ord[:, None])
    best = jnp.max(jnp.where(hits, scores, jnp.float32(-1.0)), axis=1)
    for k_a, k_b, k_m in zip(keys_a, keys_b, keys_m):
        k_lab, k_ord = k_m[0], k_m[1]
        scores = dots(k_a, k_b)
        hits = (q_lab[:, None] == k_lab[None, :]) & (k_lab[None, :] > 0) & (k_ord[None, :] < q_ord[:, None])
        best = jnp.maximum(best, jnp.max(jnp.where(hits, scores, jnp.float32(-1.0)), axis=1))

    returned = lax.all_to_all(
        best.reshape(n_grp, cap), "grp", split_axis=0, concat_axis=0, tiled=True
    ).reshape(n_slot)
    hi = lax.reduce_precision(returned, exponent_bits=8, mantissa_bits=7)
    rest = returned - hi
    mid = lax.reduce_precision(rest, exponent_bits=8, mantissa_bits=7)
    pieces = jnp.stack([hi, mid, rest - mid], axis=1).astype(jnp.bfloat16)
    got = jnp.einsum("sd,sp->dp", pick.astype(jnp.bfloat16), pieces, preferred_element_type=jnp.float32)
    return (got[:, 0] + got[:, 1]) + got[:, 2]


def solution(mesh):
    in_specs = (
        P(("grp", "split"), None),
        P(),
        P(("grp", "split")),
        P(("grp", "split")),
        P(("grp", "split")),
    )
    out_specs = P(("grp", "split"))
    return jax.shard_map(local, mesh=mesh, in_specs=in_specs, out_specs=out_specs, check_vma=False)
```

```python
import jax
import jax.numpy as jnp
from jax import lax
from jax.sharding import PartitionSpec as P

CL_GRP = 4


EPS = 1e-06
META = 128


def embed_rows(rows, weight):
    proj = jnp.einsum("...h,he->...e", rows, weight, preferred_element_type=jnp.float32)
    scale = lax.rsqrt(jnp.sum(proj * proj, axis=-1, keepdims=True) + EPS)
    return (proj * scale).astype(jnp.bfloat16)


def gather_split(rows, n_split):
    if n_split == 4:
        cross = lax.ppermute(rows, "split", [(0, 2), (1, 3), (2, 0), (3, 1)])
        pair = [(0, 1), (1, 0), (2, 3), (3, 2)]
        return [cross, lax.ppermute(rows, "split", pair), lax.ppermute(cross, "split", pair)]
    return [
        lax.ppermute(rows, "split", [(i, (i + d) % n_split) for i in range(n_split)])
        for d in range(1, n_split)
    ]


def unpack(buf, emb_w, n_all):
    emb = buf[:, :emb_w]
    lab = buf[:, emb_w].astype(jnp.float32)
    digits = [buf[:, emb_w + i].astype(jnp.float32) for i in (1, 2, 3)]
    return emb, lab, (digits[0] * n_all + digits[1] * 256.0) + digits[2]


def local(states, weight, cluster_id, block, order):
    n_doc = states.shape[0]
    n_grp = lax.axis_size("grp")
    n_split = lax.axis_size("split")
    n_dev = n_grp * n_split
    n_all = n_doc * n_dev
    cap = n_split * max(2, 2 * n_doc // n_dev)
    n_slot = n_grp * cap
    owner_of = cluster_id // CL_GRP
    onehot = (owner_of[:, None] == jnp.arange(n_grp, dtype=jnp.int32)[None, :]).astype(jnp.bfloat16)
    lower = (jnp.arange(n_doc)[:, None] > jnp.arange(n_doc)[None, :]).astype(jnp.bfloat16)
    before = jnp.dot(lower, onehot, preferred_element_type=jnp.float32)
    slot = jnp.sum(before * onehot.astype(jnp.float32), axis=1).astype(jnp.int32)
    place = owner_of * cap + slot

    embeds = embed_rows(states, weight)
    emb_w = embeds.shape[1]
    half = emb_w // 2
    label = (cluster_id - owner_of * CL_GRP + 1).astype(jnp.float32)
    digits = [label, block.astype(jnp.float32), (order // 256).astype(jnp.float32), (order % 256).astype(jnp.float32)]
    mcol = jnp.arange(META, dtype=jnp.int32)[None, :]
    meta = jnp.zeros((n_doc, META), jnp.float32)
    for i, d in enumerate(digits):
        meta = jnp.where(mcol == i, d[:, None], meta)
    meta = meta.astype(jnp.bfloat16)
    pick = place[None, :] == jnp.arange(n_slot, dtype=jnp.int32)[:, None]

    def route(rows):
        send = jnp.dot(pick.astype(jnp.bfloat16), rows, preferred_element_type=jnp.float32)
        send = send.astype(jnp.bfloat16).reshape(n_grp, cap, -1)
        got = lax.all_to_all(send, "grp", split_axis=0, concat_axis=0, tiled=True)
        return got.reshape(n_slot, -1)

    if n_split == 4:
        half = emb_w - 3 * emb_w // 8
        cross = [(0, 2), (2, 0), (1, 3), (3, 1)]
        pair = [(0, 1), (1, 0), (2, 3), (3, 2)]
        raw_b = embeds[:, half:]
        par_b = lax.ppermute(raw_b, "split", cross)
        par_place = lax.ppermute(place, "split", cross)
        col = jnp.arange(half + META, dtype=jnp.int32)[None, :]
        rows_a = jnp.where(
            col < half,
            jnp.pad(embeds[:, :half], ((0, 0), (0, META))),
            jnp.pad(meta, ((0, 0), (half, 0))),
        )
        got_a = route(rows_a)
        q_emb, q_lab, q_ord = unpack(got_a, half, n_all)
        keys_m = gather_split(jnp.stack([q_lab, q_ord]), n_split)
        pick_par = par_place[None, :] == jnp.arange(n_slot, dtype=jnp.int32)[:, None]
        send_own = jnp.dot(pick.astype(jnp.bfloat16), raw_b, preferred_element_type=jnp.float32)
        send_par = jnp.dot(pick_par.astype(jnp.bfloat16), par_b, preferred_element_type=jnp.float32)
        send = jnp.concatenate(
            [send_own.reshape(n_grp, cap, -1), send_par.reshape(n_grp, cap, -1)], axis=1
        ).astype(jnp.bfloat16)
        q_emb, send = lax.optimization_barrier((q_emb, send))
        keys_a = gather_split(q_emb, n_split)
        got = lax.all_to_all(send, "grp", split_axis=0, concat_axis=0, tiled=True)
        got_b = got[:, :cap].reshape(n_slot, -1)
        cross_b = got[:, cap:].reshape(n_slot, -1)
        keys_b = [cross_b, lax.ppermute(got_b, "split", pair), lax.ppermute(cross_b, "split", pair)]
    else:
        half = emb_w // 2
        got_a = route(jnp.concatenate([embeds[:, :half], meta], axis=1))
        q_emb, q_lab, q_ord = unpack(got_a, half, n_all)
        keys_a = gather_split(q_emb, n_split)
        keys_m = gather_split(jnp.stack([q_lab, q_ord]), n_split)
        got_b = route(embeds[:, half:])
        keys_b = gather_split(got_b, n_split)

    def dots(k_a, k_b):
        s = jnp.einsum("qe,ke->qk", q_emb, k_a, preferred_element_type=jnp.float32)
        return s + jnp.einsum("qe,ke->qk", got_b, k_b, preferred_element_type=jnp.float32)

    scores = dots(q_emb, got_b)
    hits = (q_lab[:, None] == q_lab[None, :]) & (q_lab[None, :] > 0) & (q_ord[None, :] < q_ord[:, None])
    best = jnp.max(jnp.where(hits, scores, jnp.float32(-1.0)), axis=1)
    for k_a, k_b, k_m in zip(keys_a, keys_b, keys_m):
        k_lab, k_ord = k_m[0], k_m[1]
        scores = dots(k_a, k_b)
        hits = (q_lab[:, None] == k_lab[None, :]) & (k_lab[None, :] > 0) & (k_ord[None, :] < q_ord[:, None])
        best = jnp.maximum(best, jnp.max(jnp.where(hits, scores, jnp.float32(-1.0)), axis=1))

    returned = lax.all_to_all(
        best.reshape(n_grp, cap), "grp", split_axis=0, concat_axis=0, tiled=True
    ).reshape(n_slot)
    hi = lax.reduce_precision(returned, exponent_bits=8, mantissa_bits=7)
    rest = returned - hi
    mid = lax.reduce_precision(rest, exponent_bits=8, mantissa_bits=7)
    pieces = jnp.stack([hi, mid, rest - mid], axis=1).astype(jnp.bfloat16)
    got = jnp.einsum("sd,sp->dp", pick.astype(jnp.bfloat16), pieces, preferred_element_type=jnp.float32)
    return (got[:, 0] + got[:, 1]) + got[:, 2]


def solution(mesh):
    in_specs = (
        P(("grp", "split"), None),
        P(),
        P(("grp", "split")),
        P(("grp", "split")),
        P(("grp", "split")),
    )
    out_specs = P(("grp", "split"))
    return jax.shard_map(local, mesh=mesh, in_specs=in_specs, out_specs=out_specs, check_vma=False)
```

```python
import jax
import jax.numpy as jnp
from jax import lax
from jax.sharding import PartitionSpec as P

CL_GRP = 4


EPS = 1e-06
META = 128


def embed_rows(rows, weight):
    proj = jnp.einsum("...h,he->...e", rows, weight, preferred_element_type=jnp.float32)
    scale = lax.rsqrt(jnp.sum(proj * proj, axis=-1, keepdims=True) + EPS)
    return (proj * scale).astype(jnp.bfloat16)


def gather_split(rows, n_split):
    if n_split == 4:
        cross = lax.ppermute(rows, "split", [(0, 2), (1, 3), (2, 0), (3, 1)])
        pair = [(0, 1), (1, 0), (2, 3), (3, 2)]
        return [cross, lax.ppermute(rows, "split", pair), lax.ppermute(cross, "split", pair)]
    return [
        lax.ppermute(rows, "split", [(i, (i + d) % n_split) for i in range(n_split)])
        for d in range(1, n_split)
    ]


def unpack(buf, emb_w, n_all):
    emb = buf[:, :emb_w]
    lab = buf[:, emb_w].astype(jnp.float32)
    digits = [buf[:, emb_w + i].astype(jnp.float32) for i in (1, 2, 3)]
    return emb, lab, (digits[0] * n_all + digits[1] * 256.0) + digits[2]


def local(states, weight, cluster_id, block, order):
    n_doc = states.shape[0]
    n_grp = lax.axis_size("grp")
    n_split = lax.axis_size("split")
    n_dev = n_grp * n_split
    n_all = n_doc * n_dev
    cap = n_split * max(2, 2 * n_doc // n_dev)
    n_slot = n_grp * cap
    owner_of = cluster_id // CL_GRP
    onehot = (owner_of[:, None] == jnp.arange(n_grp, dtype=jnp.int32)[None, :]).astype(jnp.bfloat16)
    lower = (jnp.arange(n_doc)[:, None] > jnp.arange(n_doc)[None, :]).astype(jnp.bfloat16)
    before = jnp.dot(lower, onehot, preferred_element_type=jnp.float32)
    slot = jnp.sum(before * onehot.astype(jnp.float32), axis=1).astype(jnp.int32)
    place = owner_of * cap + slot

    embeds = embed_rows(states, weight)
    emb_w = embeds.shape[1]
    half = emb_w // 2
    label = (cluster_id - owner_of * CL_GRP + 1).astype(jnp.float32)
    digits = [label, block.astype(jnp.float32), (order // 256).astype(jnp.float32), (order % 256).astype(jnp.float32)]
    mcol = jnp.arange(META, dtype=jnp.int32)[None, :]
    meta = jnp.zeros((n_doc, META), jnp.float32)
    for i, d in enumerate(digits):
        meta = jnp.where(mcol == i, d[:, None], meta)
    meta = meta.astype(jnp.bfloat16)
    pick = place[None, :] == jnp.arange(n_slot, dtype=jnp.int32)[:, None]

    def route(rows):
        send = jnp.dot(pick.astype(jnp.bfloat16), rows, preferred_element_type=jnp.float32)
        send = send.astype(jnp.bfloat16).reshape(n_grp, cap, -1)
        got = lax.all_to_all(send, "grp", split_axis=0, concat_axis=0, tiled=True)
        return got.reshape(n_slot, -1)

    if n_split == 4:
        half = emb_w - 3 * emb_w // 8
        cross = [(0, 2), (2, 0), (1, 3), (3, 1)]
        pair = [(0, 1), (1, 0), (2, 3), (3, 2)]
        raw_b = embeds[:, half:]
        par_b = lax.ppermute(raw_b, "split", cross)
        par_place = lax.ppermute(place, "split", cross)
        col = jnp.arange(half + META, dtype=jnp.int32)[None, :]
        rows_a = jnp.where(
            col < half,
            jnp.pad(embeds[:, :half], ((0, 0), (0, META))),
            jnp.pad(meta, ((0, 0), (half, 0))),
        )
        got_a = route(rows_a)
        q_emb, q_lab, q_ord = unpack(got_a, half, n_all)
        keys_a = gather_split(q_emb, n_split)
        keys_m = gather_split(jnp.stack([q_lab, q_ord]), n_split)
        pick_par = par_place[None, :] == jnp.arange(n_slot, dtype=jnp.int32)[:, None]
        send_own = jnp.dot(pick.astype(jnp.bfloat16), raw_b, preferred_element_type=jnp.float32)
        send_par = jnp.dot(pick_par.astype(jnp.bfloat16), par_b, preferred_element_type=jnp.float32)
        send = jnp.concatenate(
            [send_own.reshape(n_grp, cap, -1), send_par.reshape(n_grp, cap, -1)], axis=1
        ).astype(jnp.bfloat16)
        got = lax.all_to_all(send, "grp", split_axis=0, concat_axis=0, tiled=True)
        got_b = got[:, :cap].reshape(n_slot, -1)
        cross_b = got[:, cap:].reshape(n_slot, -1)
        keys_b = [cross_b, lax.ppermute(got_b, "split", pair), lax.ppermute(cross_b, "split", pair)]
    else:
        half = emb_w // 2
        got_a = route(jnp.concatenate([embeds[:, :half], meta], axis=1))
        q_emb, q_lab, q_ord = unpack(got_a, half, n_all)
        keys_a = gather_split(q_emb, n_split)
        keys_m = gather_split(jnp.stack([q_lab, q_ord]), n_split)
        got_b = route(embeds[:, half:])
        keys_b = gather_split(got_b, n_split)

    def dots(k_a, k_b):
        s = jnp.einsum("qe,ke->qk", q_emb, k_a, preferred_element_type=jnp.float32)
        return s + jnp.einsum("qe,ke->qk", got_b, k_b, preferred_element_type=jnp.float32)

    q_base = q_lab * 1048576.0
    q_code = q_base + q_ord

    def block_best(scores, k_lab, k_ord):
        k_code = k_lab * 1048576.0 + k_ord
        hits = (k_code[None, :] >= q_base[:, None]) & (k_code[None, :] < q_code[:, None])
        return jnp.max(jnp.where(hits, scores, jnp.float32(-1.0)), axis=1)

    best = block_best(dots(q_emb, got_b), q_lab, q_ord)
    for k_a, k_b, k_m in zip(keys_a, keys_b, keys_m):
        best = jnp.maximum(best, block_best(dots(k_a, k_b), k_m[0], k_m[1]))

    returned = lax.all_to_all(
        best.reshape(n_grp, cap), "grp", split_axis=0, concat_axis=0, tiled=True
    ).reshape(n_slot)
    return jnp.max(jnp.where(pick, returned[:, None], -jnp.inf), axis=0)


def solution(mesh):
    in_specs = (
        P(("grp", "split"), None),
        P(),
        P(("grp", "split")),
        P(("grp", "split")),
        P(("grp", "split")),
    )
    out_specs = P(("grp", "split"))
    return jax.shard_map(local, mesh=mesh, in_specs=in_specs, out_specs=out_specs, check_vma=False)
```

```python
import jax
import jax.numpy as jnp
from jax import lax
from jax.sharding import PartitionSpec as P

CL_GRP = 4


EPS = 1e-06
META = 128


def embed_rows(rows, weight):
    proj = jnp.einsum("...h,he->...e", rows, weight, preferred_element_type=jnp.float32)
    scale = lax.rsqrt(jnp.sum(proj * proj, axis=-1, keepdims=True) + EPS)
    return (proj * scale).astype(jnp.bfloat16)


def gather_split(rows, n_split):
    if n_split == 4:
        cross = lax.ppermute(rows, "split", [(0, 2), (1, 3), (2, 0), (3, 1)])
        pair = [(0, 1), (1, 0), (2, 3), (3, 2)]
        return [cross, lax.ppermute(rows, "split", pair), lax.ppermute(cross, "split", pair)]
    return [
        lax.ppermute(rows, "split", [(i, (i + d) % n_split) for i in range(n_split)])
        for d in range(1, n_split)
    ]


def unpack(buf, emb_w, n_all):
    emb = buf[:, :emb_w]
    lab = buf[:, emb_w].astype(jnp.float32)
    digits = [buf[:, emb_w + i].astype(jnp.float32) for i in (1, 2, 3)]
    return emb, lab, (digits[0] * n_all + digits[1] * 256.0) + digits[2]


def local(states, weight, cluster_id, block, order):
    n_doc = states.shape[0]
    n_grp = lax.axis_size("grp")
    n_split = lax.axis_size("split")
    n_dev = n_grp * n_split
    n_all = n_doc * n_dev
    cap = n_split * max(2, 2 * n_doc // n_dev)
    n_slot = n_grp * cap
    owner_of = cluster_id // CL_GRP
    onehot = (owner_of[:, None] == jnp.arange(n_grp, dtype=jnp.int32)[None, :]).astype(jnp.bfloat16)
    lower = (jnp.arange(n_doc)[:, None] > jnp.arange(n_doc)[None, :]).astype(jnp.bfloat16)
    before = jnp.dot(lower, onehot, preferred_element_type=jnp.float32)
    slot = jnp.sum(before * onehot.astype(jnp.float32), axis=1).astype(jnp.int32)
    place = owner_of * cap + slot

    embeds = embed_rows(states, weight)
    emb_w = embeds.shape[1]
    half = emb_w // 2
    label = (cluster_id - owner_of * CL_GRP + 1).astype(jnp.float32)
    digits = [label, block.astype(jnp.float32), (order // 256).astype(jnp.float32), (order % 256).astype(jnp.float32)]
    mcol = jnp.arange(META, dtype=jnp.int32)[None, :]
    meta = jnp.zeros((n_doc, META), jnp.float32)
    for i, d in enumerate(digits):
        meta = jnp.where(mcol == i, d[:, None], meta)
    meta = meta.astype(jnp.bfloat16)
    pick = place[None, :] == jnp.arange(n_slot, dtype=jnp.int32)[:, None]

    def route(rows):
        send = jnp.dot(pick.astype(jnp.bfloat16), rows, preferred_element_type=jnp.float32)
        send = send.astype(jnp.bfloat16).reshape(n_grp, cap, -1)
        got = lax.all_to_all(send, "grp", split_axis=0, concat_axis=0, tiled=True)
        return got.reshape(n_slot, -1)

    if n_split == 4:
        half = emb_w - 3 * emb_w // 8
        cross = [(0, 2), (2, 0), (1, 3), (3, 1)]
        pair = [(0, 1), (1, 0), (2, 3), (3, 2)]
        raw_b = embeds[:, half:]
        par_b = lax.ppermute(raw_b, "split", cross)
        par_place = lax.ppermute(place, "split", cross)
        col = jnp.arange(half + META, dtype=jnp.int32)[None, :]
        rows_a = jnp.where(
            col < half,
            jnp.pad(embeds[:, :half], ((0, 0), (0, META))),
            jnp.pad(meta, ((0, 0), (half, 0))),
        )
        got_a = route(rows_a)
        q_emb, q_lab, q_ord = unpack(got_a, half, n_all)
        own_m = jnp.stack([q_lab, q_ord])
        keys_a = [lax.ppermute(q_emb, "split", cross), lax.ppermute(q_emb, "split", pair)]
        keys_m = [lax.ppermute(own_m, "split", cross), lax.ppermute(own_m, "split", pair)]
        pick_par = par_place[None, :] == jnp.arange(n_slot, dtype=jnp.int32)[:, None]
        send_own = jnp.dot(pick.astype(jnp.bfloat16), raw_b, preferred_element_type=jnp.float32)
        send_par = jnp.dot(pick_par.astype(jnp.bfloat16), par_b, preferred_element_type=jnp.float32)
        send = jnp.concatenate(
            [send_own.reshape(n_grp, cap, -1), send_par.reshape(n_grp, cap, -1)], axis=1
        ).astype(jnp.bfloat16)
        got = lax.all_to_all(send, "grp", split_axis=0, concat_axis=0, tiled=True)
        got_b = got[:, :cap].reshape(n_slot, -1)
        cross_b = got[:, cap:].reshape(n_slot, -1)
        keys_b = [cross_b, lax.ppermute(got_b, "split", pair)]
    else:
        half = emb_w // 2
        got_a = route(jnp.concatenate([embeds[:, :half], meta], axis=1))
        q_emb, q_lab, q_ord = unpack(got_a, half, n_all)
        keys_a = gather_split(q_emb, n_split)
        keys_m = gather_split(jnp.stack([q_lab, q_ord]), n_split)
        got_b = route(embeds[:, half:])
        keys_b = gather_split(got_b, n_split)

    def block_best(qa, qb, qm, ka, kb, km):
        scores = jnp.einsum("qe,ke->qk", qa, ka, preferred_element_type=jnp.float32)
        scores = scores + jnp.einsum("qe,ke->qk", qb, kb, preferred_element_type=jnp.float32)
        hits = (qm[0][:, None] == km[0][None, :]) & (km[0][None, :] > 0) & (km[1][None, :] < qm[1][:, None])
        return jnp.max(jnp.where(hits, scores, jnp.float32(-1.0)), axis=1)

    mine = (q_emb, got_b, jnp.stack([q_lab, q_ord]))
    best = block_best(*mine, *mine)
    for k_a, k_b, k_m in zip(keys_a, keys_b, keys_m):
        best = jnp.maximum(best, block_best(*mine, k_a, k_b, k_m))
    if n_split == 4:
        near = (keys_a[1], keys_b[1], keys_m[1])
        far = (keys_a[0], keys_b[0], keys_m[0])
        best = jnp.maximum(best, lax.ppermute(block_best(*near, *far), "split", pair))

    returned = lax.all_to_all(
        best.reshape(n_grp, cap), "grp", split_axis=0, concat_axis=0, tiled=True
    ).reshape(n_slot)
    return jnp.max(jnp.where(pick, returned[:, None], -jnp.inf), axis=0)


def solution(mesh):
    in_specs = (
        P(("grp", "split"), None),
        P(),
        P(("grp", "split")),
        P(("grp", "split")),
        P(("grp", "split")),
    )
    out_specs = P(("grp", "split"))
    return jax.shard_map(local, mesh=mesh, in_specs=in_specs, out_specs=out_specs, check_vma=False)
```

```python
import jax
import jax.numpy as jnp
from jax import lax
from jax.sharding import PartitionSpec as P

CL_GRP = 4


EPS = 1e-06
META = 128


def embed_rows(rows, weight):
    proj = jnp.einsum("...h,he->...e", rows, weight, preferred_element_type=jnp.float32)
    scale = lax.rsqrt(jnp.sum(proj * proj, axis=-1, keepdims=True) + EPS)
    return (proj * scale).astype(jnp.bfloat16)


def gather_split(rows, n_split):
    if n_split == 4:
        cross = lax.ppermute(rows, "split", [(0, 2), (1, 3), (2, 0), (3, 1)])
        pair = [(0, 1), (1, 0), (2, 3), (3, 2)]
        return [cross, lax.ppermute(rows, "split", pair), lax.ppermute(cross, "split", pair)]
    return [
        lax.ppermute(rows, "split", [(i, (i + d) % n_split) for i in range(n_split)])
        for d in range(1, n_split)
    ]


def unpack(buf, emb_w, n_all):
    emb = buf[:, :emb_w]
    lab = buf[:, emb_w].astype(jnp.float32)
    digits = [buf[:, emb_w + i].astype(jnp.float32) for i in (1, 2, 3)]
    return emb, lab, (digits[0] * n_all + digits[1] * 256.0) + digits[2]


def local(states, weight, cluster_id, block, order):
    n_doc = states.shape[0]
    n_grp = lax.axis_size("grp")
    n_split = lax.axis_size("split")
    n_dev = n_grp * n_split
    n_all = n_doc * n_dev
    cap = n_split * max(2, 2 * n_doc // n_dev)
    n_slot = n_grp * cap
    owner_of = cluster_id // CL_GRP
    onehot = (owner_of[:, None] == jnp.arange(n_grp, dtype=jnp.int32)[None, :]).astype(jnp.bfloat16)
    lower = (jnp.arange(n_doc)[:, None] > jnp.arange(n_doc)[None, :]).astype(jnp.bfloat16)
    before = jnp.dot(lower, onehot, preferred_element_type=jnp.float32)
    slot = jnp.sum(before * onehot.astype(jnp.float32), axis=1).astype(jnp.int32)
    place = owner_of * cap + slot

    embeds = embed_rows(states, weight)
    emb_w = embeds.shape[1]
    half = emb_w // 2
    label = (cluster_id - owner_of * CL_GRP + 1).astype(jnp.float32)
    digits = [label, block.astype(jnp.float32), (order // 256).astype(jnp.float32), (order % 256).astype(jnp.float32)]
    mcol = jnp.arange(META, dtype=jnp.int32)[None, :]
    meta = jnp.zeros((n_doc, META), jnp.float32)
    for i, d in enumerate(digits):
        meta = jnp.where(mcol == i, d[:, None], meta)
    meta = meta.astype(jnp.bfloat16)
    pick = place[None, :] == jnp.arange(n_slot, dtype=jnp.int32)[:, None]

    def route(rows):
        send = jnp.dot(pick.astype(jnp.bfloat16), rows, preferred_element_type=jnp.float32)
        send = send.astype(jnp.bfloat16).reshape(n_grp, cap, -1)
        got = lax.all_to_all(send, "grp", split_axis=0, concat_axis=0, tiled=True)
        return got.reshape(n_slot, -1)

    if n_split == 4:
        half = emb_w - 3 * emb_w // 8
        cross = [(0, 2), (2, 0), (1, 3), (3, 1)]
        pair = [(0, 1), (1, 0), (2, 3), (3, 2)]
        raw_b = embeds[:, half:]
        par_b = lax.ppermute(raw_b, "split", cross)
        par_place = lax.ppermute(place, "split", cross)
        col = jnp.arange(half + META, dtype=jnp.int32)[None, :]
        rows_a = jnp.where(
            col < half,
            jnp.pad(embeds[:, :half], ((0, 0), (0, META))),
            jnp.pad(meta, ((0, 0), (half, 0))),
        )
        got_a = route(rows_a)
        q_emb, q_lab, q_ord = unpack(got_a, half, n_all)
        own_m = jnp.stack([q_lab, q_ord])
        keys_a = [lax.ppermute(q_emb, "split", cross), lax.ppermute(q_emb, "split", pair)]
        keys_m = [lax.ppermute(own_m, "split", cross), lax.ppermute(own_m, "split", pair)]
        pick_par = par_place[None, :] == jnp.arange(n_slot, dtype=jnp.int32)[:, None]
        send_own = jnp.dot(pick.astype(jnp.bfloat16), raw_b, preferred_element_type=jnp.float32)
        send_par = jnp.dot(pick_par.astype(jnp.bfloat16), par_b, preferred_element_type=jnp.float32)
        send = jnp.concatenate(
            [send_own.reshape(n_grp, cap, -1), send_par.reshape(n_grp, cap, -1)], axis=1
        ).astype(jnp.bfloat16)
        got = lax.all_to_all(send, "grp", split_axis=0, concat_axis=0, tiled=True)
        got_b = got[:, :cap].reshape(n_slot, -1)
        cross_b = got[:, cap:].reshape(n_slot, -1)
        keys_b = [cross_b, lax.ppermute(got_b, "split", pair)]
    else:
        half = emb_w // 2
        got_a = route(jnp.concatenate([embeds[:, :half], meta], axis=1))
        q_emb, q_lab, q_ord = unpack(got_a, half, n_all)
        keys_a = gather_split(q_emb, n_split)
        keys_m = gather_split(jnp.stack([q_lab, q_ord]), n_split)
        got_b = route(embeds[:, half:])
        keys_b = gather_split(got_b, n_split)

    def block_best(qa, qb, qm, ka, kb, km):
        scores = jnp.einsum("qe,ke->qk", qa, ka, preferred_element_type=jnp.float32)
        scores = scores + jnp.einsum("qe,ke->qk", qb, kb, preferred_element_type=jnp.float32)
        hits = (qm[0][:, None] == km[0][None, :]) & (km[0][None, :] > 0) & (km[1][None, :] < qm[1][:, None])
        return jnp.max(jnp.where(hits, scores, jnp.float32(-1.0)), axis=1)

    def early_best(qa, qb, qm, ka, kb, km):
        scores = jnp.einsum("qe,ke->qk", qa, ka, preferred_element_type=jnp.float32)
        hits = (qm[0][:, None] == km[0][None, :]) & (km[0][None, :] > 0) & (km[1][None, :] < qm[1][:, None])
        masked = lax.optimization_barrier(jnp.where(hits, scores, -jnp.inf))
        scores = masked + jnp.einsum("qe,ke->qk", qb, kb, preferred_element_type=jnp.float32)
        return jnp.maximum(jnp.max(scores, axis=1), jnp.float32(-1.0))

    mine = (q_emb, got_b, jnp.stack([q_lab, q_ord]))
    blocks = list(zip(keys_a, keys_b, keys_m))
    if n_split == 4:
        best = jnp.maximum(early_best(*mine, *mine), early_best(*mine, *blocks[1]))
        best = jnp.maximum(best, block_best(*mine, *blocks[0]))
    else:
        best = block_best(*mine, *mine)
        for k_a, k_b, k_m in blocks:
            best = jnp.maximum(best, block_best(*mine, k_a, k_b, k_m))
    if n_split == 4:
        near = (keys_a[1], keys_b[1], keys_m[1])
        far = (keys_a[0], keys_b[0], keys_m[0])
        best = jnp.maximum(best, lax.ppermute(block_best(*near, *far), "split", pair))

    returned = lax.all_to_all(
        best.reshape(n_grp, cap), "grp", split_axis=0, concat_axis=0, tiled=True
    ).reshape(n_slot)
    return jnp.max(jnp.where(pick, returned[:, None], -jnp.inf), axis=0)


def solution(mesh):
    in_specs = (
        P(("grp", "split"), None),
        P(),
        P(("grp", "split")),
        P(("grp", "split")),
        P(("grp", "split")),
    )
    out_specs = P(("grp", "split"))
    return jax.shard_map(local, mesh=mesh, in_specs=in_specs, out_specs=out_specs, check_vma=False)
```

```python
import jax
import jax.numpy as jnp
from jax import lax
from jax.sharding import PartitionSpec as P

CL_GRP = 4


EPS = 1e-06
META = 128


def embed_rows(rows, weight):
    proj = jnp.einsum("...h,he->...e", rows, weight, preferred_element_type=jnp.float32)
    scale = lax.rsqrt(jnp.sum(proj * proj, axis=-1, keepdims=True) + EPS)
    return (proj * scale).astype(jnp.bfloat16)


def gather_split(rows, n_split):
    if n_split == 4:
        cross = lax.ppermute(rows, "split", [(0, 2), (1, 3), (2, 0), (3, 1)])
        pair = [(0, 1), (1, 0), (2, 3), (3, 2)]
        return [cross, lax.ppermute(rows, "split", pair), lax.ppermute(cross, "split", pair)]
    return [
        lax.ppermute(rows, "split", [(i, (i + d) % n_split) for i in range(n_split)])
        for d in range(1, n_split)
    ]


def unpack(buf, emb_w, n_all):
    emb = buf[:, :emb_w]
    lab = buf[:, emb_w].astype(jnp.float32)
    digits = [buf[:, emb_w + i].astype(jnp.float32) for i in (1, 2, 3)]
    return emb, lab, (digits[0] * n_all + digits[1] * 256.0) + digits[2]


def local(states, weight, cluster_id, block, order):
    n_doc = states.shape[0]
    n_grp = lax.axis_size("grp")
    n_split = lax.axis_size("split")
    n_dev = n_grp * n_split
    n_all = n_doc * n_dev
    cap = n_split * max(2, 2 * n_doc // n_dev)
    n_slot = n_grp * cap
    owner_of = cluster_id // CL_GRP
    onehot = (owner_of[:, None] == jnp.arange(n_grp, dtype=jnp.int32)[None, :]).astype(jnp.bfloat16)
    lower = (jnp.arange(n_doc)[:, None] > jnp.arange(n_doc)[None, :]).astype(jnp.bfloat16)
    before = jnp.dot(lower, onehot, preferred_element_type=jnp.float32)
    slot = jnp.sum(before * onehot.astype(jnp.float32), axis=1).astype(jnp.int32)
    place = owner_of * cap + slot

    embeds = embed_rows(states, weight)
    emb_w = embeds.shape[1]
    half = emb_w // 2
    label = (cluster_id - owner_of * CL_GRP + 1).astype(jnp.float32)
    digits = [label, block.astype(jnp.float32), (order // 256).astype(jnp.float32), (order % 256).astype(jnp.float32)]
    mcol = jnp.arange(META, dtype=jnp.int32)[None, :]
    meta = jnp.zeros((n_doc, META), jnp.float32)
    for i, d in enumerate(digits):
        meta = jnp.where(mcol == i, d[:, None], meta)
    meta = meta.astype(jnp.bfloat16)
    pick = place[None, :] == jnp.arange(n_slot, dtype=jnp.int32)[:, None]

    def route(rows):
        send = jnp.dot(pick.astype(jnp.bfloat16), rows, preferred_element_type=jnp.float32)
        send = send.astype(jnp.bfloat16).reshape(n_grp, cap, -1)
        got = lax.all_to_all(send, "grp", split_axis=0, concat_axis=0, tiled=True)
        return got.reshape(n_slot, -1)

    if n_split == 4:
        half = emb_w - 3 * emb_w // 8
        cross = [(0, 2), (2, 0), (1, 3), (3, 1)]
        pair = [(0, 1), (1, 0), (2, 3), (3, 2)]
        raw_b = embeds[:, half:]
        par_b = lax.ppermute(raw_b, "split", cross)
        par_place = lax.ppermute(place, "split", cross)
        col = jnp.arange(half + META, dtype=jnp.int32)[None, :]
        rows_a = jnp.where(
            col < half,
            jnp.pad(embeds[:, :half], ((0, 0), (0, META))),
            jnp.pad(meta, ((0, 0), (half, 0))),
        )
        got_a = route(rows_a)
        q_emb, q_lab, q_ord = unpack(got_a, half, n_all)
        own_m = jnp.stack([q_lab, q_ord])
        keys_a = [lax.ppermute(q_emb, "split", cross), lax.ppermute(q_emb, "split", pair)]
        keys_m = [lax.ppermute(own_m, "split", cross), lax.ppermute(own_m, "split", pair)]
        pick_par = par_place[None, :] == jnp.arange(n_slot, dtype=jnp.int32)[:, None]
        send_own = jnp.dot(pick.astype(jnp.bfloat16), raw_b, preferred_element_type=jnp.float32)
        send_par = jnp.dot(pick_par.astype(jnp.bfloat16), par_b, preferred_element_type=jnp.float32)
        send = jnp.stack(
            [send_own.reshape(n_grp, cap, -1), send_par.reshape(n_grp, cap, -1)], axis=0
        ).astype(jnp.bfloat16)
        got = lax.all_to_all(send, "grp", split_axis=1, concat_axis=1, tiled=True)
        got_b = got[0].reshape(n_slot, -1)
        cross_b = got[1].reshape(n_slot, -1)
        keys_b = [cross_b, lax.ppermute(got_b, "split", pair)]
    else:
        half = emb_w // 2
        got_a = route(jnp.concatenate([embeds[:, :half], meta], axis=1))
        q_emb, q_lab, q_ord = unpack(got_a, half, n_all)
        keys_a = gather_split(q_emb, n_split)
        keys_m = gather_split(jnp.stack([q_lab, q_ord]), n_split)
        got_b = route(embeds[:, half:])
        keys_b = gather_split(got_b, n_split)

    def block_best(qa, qb, qm, ka, kb, km):
        scores = jnp.einsum("qe,ke->qk", qa, ka, preferred_element_type=jnp.float32)
        scores = scores + jnp.einsum("qe,ke->qk", qb, kb, preferred_element_type=jnp.float32)
        hits = (qm[0][:, None] == km[0][None, :]) & (km[0][None, :] > 0) & (km[1][None, :] < qm[1][:, None])
        return jnp.max(jnp.where(hits, scores, jnp.float32(-1.0)), axis=1)

    mine = (q_emb, got_b, jnp.stack([q_lab, q_ord]))
    best = block_best(*mine, *mine)
    for k_a, k_b, k_m in zip(keys_a, keys_b, keys_m):
        best = jnp.maximum(best, block_best(*mine, k_a, k_b, k_m))
    if n_split == 4:
        near = (keys_a[1], keys_b[1], keys_m[1])
        far = (keys_a[0], keys_b[0], keys_m[0])
        best = jnp.maximum(best, lax.ppermute(block_best(*near, *far), "split", pair))

    returned = lax.all_to_all(
        best.reshape(n_grp, cap), "grp", split_axis=0, concat_axis=0, tiled=True
    ).reshape(n_slot)
    return jnp.max(jnp.where(pick, returned[:, None], -jnp.inf), axis=0)


def solution(mesh):
    in_specs = (
        P(("grp", "split"), None),
        P(),
        P(("grp", "split")),
        P(("grp", "split")),
        P(("grp", "split")),
    )
    out_specs = P(("grp", "split"))
    return jax.shard_map(local, mesh=mesh, in_specs=in_specs, out_specs=out_specs, check_vma=False)
```

```python
import jax
import jax.numpy as jnp
from jax import lax
from jax.sharding import PartitionSpec as P

CL_GRP = 4


EPS = 1e-06
META = 128


def embed_rows(rows, weight):
    proj = jnp.einsum("...h,he->...e", rows, weight, preferred_element_type=jnp.float32)
    scale = lax.rsqrt(jnp.sum(proj * proj, axis=-1, keepdims=True) + EPS)
    return (proj * scale).astype(jnp.bfloat16)


def gather_split(rows, n_split):
    if n_split == 4:
        cross = lax.ppermute(rows, "split", [(0, 2), (1, 3), (2, 0), (3, 1)])
        pair = [(0, 1), (1, 0), (2, 3), (3, 2)]
        return [cross, lax.ppermute(rows, "split", pair), lax.ppermute(cross, "split", pair)]
    return [
        lax.ppermute(rows, "split", [(i, (i + d) % n_split) for i in range(n_split)])
        for d in range(1, n_split)
    ]


def unpack(buf, emb_w, n_all):
    emb = buf[:, :emb_w]
    lab = buf[:, emb_w].astype(jnp.float32)
    digits = [buf[:, emb_w + i].astype(jnp.float32) for i in (1, 2, 3)]
    return emb, lab, (digits[0] * n_all + digits[1] * 256.0) + digits[2]


def local(states, weight, cluster_id, block, order):
    n_doc = states.shape[0]
    n_grp = lax.axis_size("grp")
    n_split = lax.axis_size("split")
    n_dev = n_grp * n_split
    n_all = n_doc * n_dev
    cap = n_split * max(2, 2 * n_doc // n_dev)
    n_slot = n_grp * cap
    owner_of = cluster_id // CL_GRP
    onehot = (owner_of[:, None] == jnp.arange(n_grp, dtype=jnp.int32)[None, :]).astype(jnp.bfloat16)
    lower = (jnp.arange(n_doc)[:, None] > jnp.arange(n_doc)[None, :]).astype(jnp.bfloat16)
    before = jnp.dot(lower, onehot, preferred_element_type=jnp.float32)
    slot = jnp.sum(before * onehot.astype(jnp.float32), axis=1).astype(jnp.int32)
    place = owner_of * cap + slot

    embeds = embed_rows(states, weight)
    emb_w = embeds.shape[1]
    half = emb_w // 2
    label = (cluster_id - owner_of * CL_GRP + 1).astype(jnp.float32)
    digits = [label, block.astype(jnp.float32), (order // 256).astype(jnp.float32), (order % 256).astype(jnp.float32)]
    mcol = jnp.arange(META, dtype=jnp.int32)[None, :]
    meta = jnp.zeros((n_doc, META), jnp.float32)
    for i, d in enumerate(digits):
        meta = jnp.where(mcol == i, d[:, None], meta)
    meta = meta.astype(jnp.bfloat16)
    pick = place[None, :] == jnp.arange(n_slot, dtype=jnp.int32)[:, None]

    def route(rows):
        send = jnp.dot(pick.astype(jnp.bfloat16), rows, preferred_element_type=jnp.float32)
        send = send.astype(jnp.bfloat16).reshape(n_grp, cap, -1)
        got = lax.all_to_all(send, "grp", split_axis=0, concat_axis=0, tiled=True)
        return got.reshape(n_slot, -1)

    if n_split == 4:
        half = emb_w - 3 * emb_w // 8
        cross = [(0, 2), (2, 0), (1, 3), (3, 1)]
        pair = [(0, 1), (1, 0), (2, 3), (3, 2)]
        raw_b = embeds[:, half:]
        par_b = lax.ppermute(raw_b, "split", cross)
        par_place = lax.ppermute(place, "split", cross)
        col = jnp.arange(half + META, dtype=jnp.int32)[None, :]
        rows_a = jnp.where(
            col < half,
            jnp.pad(embeds[:, :half], ((0, 0), (0, META))),
            jnp.pad(meta, ((0, 0), (half, 0))),
        )
        got_a = route(rows_a)
        q_emb, q_lab, q_ord = unpack(got_a, half, n_all)
        own_m = jnp.stack([q_lab, q_ord])
        keys_a = [lax.ppermute(q_emb, "split", cross), lax.ppermute(q_emb, "split", pair)]
        keys_m = [lax.ppermute(own_m, "split", cross), lax.ppermute(own_m, "split", pair)]
        pick_par = par_place[None, :] == jnp.arange(n_slot, dtype=jnp.int32)[:, None]
        send_own = jnp.dot(pick.astype(jnp.bfloat16), raw_b, preferred_element_type=jnp.float32)
        send_par = jnp.dot(pick_par.astype(jnp.bfloat16), par_b, preferred_element_type=jnp.float32)
        send = jnp.concatenate(
            [send_own.reshape(n_grp, cap, -1), send_par.reshape(n_grp, cap, -1)], axis=1
        ).astype(jnp.bfloat16)
        got = lax.all_to_all(send, "grp", split_axis=0, concat_axis=0, tiled=True)
        got_b = got[:, :cap].reshape(n_slot, -1)
        cross_b = got[:, cap:].reshape(n_slot, -1)
        keys_b = [cross_b, lax.ppermute(got_b, "split", pair)]
    else:
        half = emb_w // 2
        got_a = route(jnp.concatenate([embeds[:, :half], meta], axis=1))
        q_emb, q_lab, q_ord = unpack(got_a, half, n_all)
        keys_a = gather_split(q_emb, n_split)
        keys_m = gather_split(jnp.stack([q_lab, q_ord]), n_split)
        got_b = route(embeds[:, half:])
        keys_b = gather_split(got_b, n_split)

    def block_best(qa, qb, qm, ka, kb, km):
        scores = jnp.einsum("qe,ke->qk", qa, ka, preferred_element_type=jnp.float32)
        scores = scores + jnp.einsum("qe,ke->qk", qb, kb, preferred_element_type=jnp.float32)
        hits = (qm[0][:, None] == km[0][None, :]) & (km[0][None, :] > 0) & (km[1][None, :] < qm[1][:, None])
        return jnp.max(jnp.where(hits, scores, jnp.float32(-1.0)), axis=1)

    mine = (q_emb, got_b, jnp.stack([q_lab, q_ord]))
    best = block_best(*mine, *mine)
    for k_a, k_b, k_m in reversed(list(zip(keys_a, keys_b, keys_m))):
        best = jnp.maximum(best, block_best(*mine, k_a, k_b, k_m))
    if n_split == 4:
        near = (keys_a[1], keys_b[1], keys_m[1])
        far = (keys_a[0], keys_b[0], keys_m[0])
        best = jnp.maximum(best, lax.ppermute(block_best(*near, *far), "split", pair))

    returned = lax.all_to_all(
        best.reshape(n_grp, cap), "grp", split_axis=0, concat_axis=0, tiled=True
    ).reshape(n_slot)
    return jnp.max(jnp.where(pick, returned[:, None], -jnp.inf), axis=0)


def solution(mesh):
    in_specs = (
        P(("grp", "split"), None),
        P(),
        P(("grp", "split")),
        P(("grp", "split")),
        P(("grp", "split")),
    )
    out_specs = P(("grp", "split"))
    return jax.shard_map(local, mesh=mesh, in_specs=in_specs, out_specs=out_specs, check_vma=False)
```

```python
import jax
import jax.numpy as jnp
from jax import lax
from jax.sharding import PartitionSpec as P

CL_GRP = 4


EPS = 1e-06
META = 128


def embed_rows(rows, weight):
    proj = jnp.einsum("...h,he->...e", rows, weight, preferred_element_type=jnp.float32)
    scale = lax.rsqrt(jnp.sum(proj * proj, axis=-1, keepdims=True) + EPS)
    return (proj * scale).astype(jnp.bfloat16)


def gather_split(rows, n_split):
    if n_split == 4:
        cross = lax.ppermute(rows, "split", [(0, 2), (1, 3), (2, 0), (3, 1)])
        pair = [(0, 1), (1, 0), (2, 3), (3, 2)]
        return [cross, lax.ppermute(rows, "split", pair), lax.ppermute(cross, "split", pair)]
    return [
        lax.ppermute(rows, "split", [(i, (i + d) % n_split) for i in range(n_split)])
        for d in range(1, n_split)
    ]


def unpack(buf, emb_w, n_all):
    emb = buf[:, :emb_w]
    lab = buf[:, emb_w].astype(jnp.float32)
    digits = [buf[:, emb_w + i].astype(jnp.float32) for i in (1, 2, 3)]
    return emb, lab, (digits[0] * n_all + digits[1] * 256.0) + digits[2]


def local(states, weight, cluster_id, block, order):
    n_doc = states.shape[0]
    n_grp = lax.axis_size("grp")
    n_split = lax.axis_size("split")
    n_dev = n_grp * n_split
    n_all = n_doc * n_dev
    cap = n_split * max(2, 2 * n_doc // n_dev)
    n_slot = n_grp * cap
    owner_of = cluster_id // CL_GRP
    onehot = (owner_of[:, None] == jnp.arange(n_grp, dtype=jnp.int32)[None, :]).astype(jnp.bfloat16)
    lower = (jnp.arange(n_doc)[:, None] > jnp.arange(n_doc)[None, :]).astype(jnp.bfloat16)
    before = jnp.dot(lower, onehot, preferred_element_type=jnp.float32)
    slot = jnp.sum(before * onehot.astype(jnp.float32), axis=1).astype(jnp.int32)
    place = owner_of * cap + slot

    embeds = embed_rows(states, weight)
    emb_w = embeds.shape[1]
    half = emb_w // 2
    label = (cluster_id - owner_of * CL_GRP + 1).astype(jnp.float32)
    digits = [label, block.astype(jnp.float32), (order // 256).astype(jnp.float32), (order % 256).astype(jnp.float32)]
    mcol = jnp.arange(META, dtype=jnp.int32)[None, :]
    meta = jnp.zeros((n_doc, META), jnp.float32)
    for i, d in enumerate(digits):
        meta = jnp.where(mcol == i, d[:, None], meta)
    meta = meta.astype(jnp.bfloat16)
    pick = place[None, :] == jnp.arange(n_slot, dtype=jnp.int32)[:, None]

    def route(rows):
        send = jnp.dot(pick.astype(jnp.bfloat16), rows, preferred_element_type=jnp.float32)
        send = send.astype(jnp.bfloat16).reshape(n_grp, cap, -1)
        got = lax.all_to_all(send, "grp", split_axis=0, concat_axis=0, tiled=True)
        return got.reshape(n_slot, -1)

    if n_split == 4:
        half = emb_w - 3 * emb_w // 8
        cross = [(0, 2), (2, 0), (1, 3), (3, 1)]
        pair = [(0, 1), (1, 0), (2, 3), (3, 2)]
        raw_b = embeds[:, half:]
        par_b = lax.ppermute(raw_b, "split", cross)
        par_place = lax.ppermute(place, "split", cross)
        col = jnp.arange(half + META, dtype=jnp.int32)[None, :]
        rows_a = jnp.where(
            col < half,
            jnp.pad(embeds[:, :half], ((0, 0), (0, META))),
            jnp.pad(meta, ((0, 0), (half, 0))),
        )
        got_a = route(rows_a)
        q_emb, q_lab, q_ord = unpack(got_a, half, n_all)
        own_m = jnp.stack([q_lab, q_ord])
        keys_a = [lax.ppermute(q_emb, "split", cross), lax.ppermute(q_emb, "split", pair)]
        keys_m = [lax.ppermute(own_m, "split", cross), lax.ppermute(own_m, "split", pair)]
        pick_par = par_place[None, :] == jnp.arange(n_slot, dtype=jnp.int32)[:, None]
        send_own = jnp.dot(pick.astype(jnp.bfloat16), raw_b, preferred_element_type=jnp.float32)
        send_par = jnp.dot(pick_par.astype(jnp.bfloat16), par_b, preferred_element_type=jnp.float32)
        send = jnp.concatenate(
            [send_own.reshape(n_grp, cap, -1), send_par.reshape(n_grp, cap, -1)], axis=1
        ).astype(jnp.bfloat16)
        got = lax.all_to_all(send, "grp", split_axis=0, concat_axis=0, tiled=True)
        got_b = got[:, :cap].reshape(n_slot, -1)
        cross_b = got[:, cap:].reshape(n_slot, -1)
        keys_b = [cross_b, lax.ppermute(got_b, "split", pair)]
    else:
        half = emb_w // 2
        got_a = route(jnp.concatenate([embeds[:, :half], meta], axis=1))
        q_emb, q_lab, q_ord = unpack(got_a, half, n_all)
        keys_a = gather_split(q_emb, n_split)
        keys_m = gather_split(jnp.stack([q_lab, q_ord]), n_split)
        got_b = route(embeds[:, half:])
        keys_b = gather_split(got_b, n_split)

    def block_best(qa, qb, qm, ka, kb, km):
        scores = jnp.einsum("qe,ke->qk", qa, ka, preferred_element_type=jnp.float32)
        scores = scores + jnp.einsum("qe,ke->qk", qb, kb, preferred_element_type=jnp.float32)
        hits = (qm[0][:, None] == km[0][None, :]) & (km[0][None, :] > 0) & (km[1][None, :] < qm[1][:, None])
        return jnp.max(jnp.where(hits, scores, jnp.float32(-1.0)), axis=1)

    mine = (q_emb, got_b, jnp.stack([q_lab, q_ord]))
    best = block_best(*mine, *mine)
    if n_split == 4:
        best = jnp.maximum(best, block_best(*mine, keys_a[1], keys_b[1], keys_m[1]))
        both = (
            jnp.concatenate([q_emb, keys_a[1]], axis=0),
            jnp.concatenate([got_b, keys_b[1]], axis=0),
            jnp.concatenate([mine[2], keys_m[1]], axis=1),
        )
        far = block_best(*both, keys_a[0], keys_b[0], keys_m[0])
        best = jnp.maximum(best, far[:n_slot])
        best = jnp.maximum(best, lax.ppermute(far[n_slot:], "split", pair))
    else:
        for k_a, k_b, k_m in zip(keys_a, keys_b, keys_m):
            best = jnp.maximum(best, block_best(*mine, k_a, k_b, k_m))

    returned = lax.all_to_all(
        best.reshape(n_grp, cap), "grp", split_axis=0, concat_axis=0, tiled=True
    ).reshape(n_slot)
    return jnp.max(jnp.where(pick, returned[:, None], -jnp.inf), axis=0)


def solution(mesh):
    in_specs = (
        P(("grp", "split"), None),
        P(),
        P(("grp", "split")),
        P(("grp", "split")),
        P(("grp", "split")),
    )
    out_specs = P(("grp", "split"))
    return jax.shard_map(local, mesh=mesh, in_specs=in_specs, out_specs=out_specs, check_vma=False)
```

```python
import jax
import jax.numpy as jnp
from jax import lax
from jax.sharding import PartitionSpec as P

CL_GRP = 4


EPS = 1e-06
META = 128


def embed_rows(rows, weight):
    proj = jnp.einsum("...h,he->...e", rows, weight, preferred_element_type=jnp.float32)
    scale = lax.rsqrt(jnp.sum(proj * proj, axis=-1, keepdims=True) + EPS)
    return (proj * scale).astype(jnp.bfloat16)


def gather_split(rows, n_split):
    if n_split == 4:
        cross = lax.ppermute(rows, "split", [(0, 2), (1, 3), (2, 0), (3, 1)])
        pair = [(0, 1), (1, 0), (2, 3), (3, 2)]
        return [cross, lax.ppermute(rows, "split", pair), lax.ppermute(cross, "split", pair)]
    return [
        lax.ppermute(rows, "split", [(i, (i + d) % n_split) for i in range(n_split)])
        for d in range(1, n_split)
    ]


def unpack(buf, emb_w, n_all):
    emb = buf[:, :emb_w]
    lab = buf[:, emb_w].astype(jnp.float32)
    digits = [buf[:, emb_w + i].astype(jnp.float32) for i in (1, 2, 3)]
    return emb, lab, (digits[0] * n_all + digits[1] * 256.0) + digits[2]


def local(states, weight, cluster_id, block, order):
    n_doc = states.shape[0]
    n_grp = lax.axis_size("grp")
    n_split = lax.axis_size("split")
    n_dev = n_grp * n_split
    n_all = n_doc * n_dev
    cap = n_split * max(2, 2 * n_doc // n_dev)
    n_slot = n_grp * cap
    owner_of = cluster_id // CL_GRP
    onehot = (owner_of[:, None] == jnp.arange(n_grp, dtype=jnp.int32)[None, :]).astype(jnp.bfloat16)
    lower = (jnp.arange(n_doc)[:, None] > jnp.arange(n_doc)[None, :]).astype(jnp.bfloat16)
    before = jnp.dot(lower, onehot, preferred_element_type=jnp.float32)
    slot = jnp.sum(before * onehot.astype(jnp.float32), axis=1).astype(jnp.int32)
    place = owner_of * cap + slot

    embeds = embed_rows(states, weight)
    emb_w = embeds.shape[1]
    half = emb_w // 2
    label = (cluster_id - owner_of * CL_GRP + 1).astype(jnp.float32)
    digits = [label, block.astype(jnp.float32), (order // 256).astype(jnp.float32), (order % 256).astype(jnp.float32)]
    mcol = jnp.arange(META, dtype=jnp.int32)[None, :]
    meta = jnp.zeros((n_doc, META), jnp.float32)
    for i, d in enumerate(digits):
        meta = jnp.where(mcol == i, d[:, None], meta)
    meta = meta.astype(jnp.bfloat16)
    pick = place[None, :] == jnp.arange(n_slot, dtype=jnp.int32)[:, None]

    def route(rows):
        send = jnp.dot(pick.astype(jnp.bfloat16), rows, preferred_element_type=jnp.float32)
        send = send.astype(jnp.bfloat16).reshape(n_grp, cap, -1)
        got = lax.all_to_all(send, "grp", split_axis=0, concat_axis=0, tiled=True)
        return got.reshape(n_slot, -1)

    if n_split == 4:
        half = emb_w - emb_w // 4
        cross = [(0, 2), (2, 0), (1, 3), (3, 1)]
        pair = [(0, 1), (1, 0), (2, 3), (3, 2)]
        raw_b = embeds[:, half:]
        par_b = lax.ppermute(raw_b, "split", cross)
        par_place = lax.ppermute(place, "split", cross)
        col = jnp.arange(half + META, dtype=jnp.int32)[None, :]
        rows_a = jnp.where(
            col < half,
            jnp.pad(embeds[:, :half], ((0, 0), (0, META))),
            jnp.pad(meta, ((0, 0), (half, 0))),
        )
        got_a = route(rows_a)
        q_emb, q_lab, q_ord = unpack(got_a, half, n_all)
        own_m = jnp.stack([q_lab, q_ord])
        keys_a = [lax.ppermute(q_emb, "split", cross), lax.ppermute(q_emb, "split", pair)]
        keys_m = [lax.ppermute(own_m, "split", cross), lax.ppermute(own_m, "split", pair)]
        pick_par = par_place[None, :] == jnp.arange(n_slot, dtype=jnp.int32)[:, None]
        send_own = jnp.dot(pick.astype(jnp.bfloat16), raw_b, preferred_element_type=jnp.float32)
        send_par = jnp.dot(pick_par.astype(jnp.bfloat16), par_b, preferred_element_type=jnp.float32)
        send = jnp.concatenate(
            [send_own.reshape(n_grp, cap, -1), send_par.reshape(n_grp, cap, -1)], axis=1
        ).astype(jnp.bfloat16)
        got = lax.all_to_all(send, "grp", split_axis=0, concat_axis=0, tiled=True)
        got_b = got[:, :cap].reshape(n_slot, -1)
        cross_b = got[:, cap:].reshape(n_slot, -1)
        keys_b = [cross_b, lax.ppermute(got_b, "split", pair)]
    else:
        half = emb_w // 2
        got_a = route(jnp.concatenate([embeds[:, :half], meta], axis=1))
        q_emb, q_lab, q_ord = unpack(got_a, half, n_all)
        keys_a = gather_split(q_emb, n_split)
        keys_m = gather_split(jnp.stack([q_lab, q_ord]), n_split)
        got_b = route(embeds[:, half:])
        keys_b = gather_split(got_b, n_split)

    def block_best(qa, qb, qm, ka, kb, km):
        scores = jnp.einsum("qe,ke->qk", qa, ka, preferred_element_type=jnp.float32)
        scores = scores + jnp.einsum("qe,ke->qk", qb, kb, preferred_element_type=jnp.float32)
        hits = (qm[0][:, None] == km[0][None, :]) & (km[0][None, :] > 0) & (km[1][None, :] < qm[1][:, None])
        return jnp.max(jnp.where(hits, scores, jnp.float32(-1.0)), axis=1)

    mine = (q_emb, got_b, jnp.stack([q_lab, q_ord]))
    best = block_best(*mine, *mine)
    for k_a, k_b, k_m in zip(keys_a, keys_b, keys_m):
        best = jnp.maximum(best, block_best(*mine, k_a, k_b, k_m))
    if n_split == 4:
        near = (keys_a[1], keys_b[1], keys_m[1])
        far = (keys_a[0], keys_b[0], keys_m[0])
        best = jnp.maximum(best, lax.ppermute(block_best(*near, *far), "split", pair))

    returned = lax.all_to_all(
        best.reshape(n_grp, cap), "grp", split_axis=0, concat_axis=0, tiled=True
    ).reshape(n_slot)
    return jnp.max(jnp.where(pick, returned[:, None], -jnp.inf), axis=0)


def solution(mesh):
    in_specs = (
        P(("grp", "split"), None),
        P(),
        P(("grp", "split")),
        P(("grp", "split")),
        P(("grp", "split")),
    )
    out_specs = P(("grp", "split"))
    return jax.shard_map(local, mesh=mesh, in_specs=in_specs, out_specs=out_specs, check_vma=False)
```
